32 devices in a mesh: rep: 2 (over x), tm: 8 (over z, y), mp: 2 (over core).
Axes of the slice: x: 2, y: 2, z: 4, core: 2. Of those that a mesh axis runs over, the one named last changes fastest.
Arguments:
- inputs: bfloat16 [8, 1024, 1024], P('rep', 'tm'), parts along dimension 0, may hold values from -6 to 6
- resets: int32 [8, 1024], P('rep', 'tm'), parts along dimension 0, may hold values 0 or 1
- actions: int32 [8, 8, 128, 4], P('rep', None, 'tm'), parts along dimension 0, may hold values from 0 to 17
- in_proj: bfloat16 [1024, 1024], P(None, 'mp'), may hold values from -0.1875 to 0.1875
- decay_rates: float32 [1024], replicated, may hold values from 0.00024414062 to 0.03
- readout_w: bfloat16 [1024, 1024], P('mp'), may hold values from -0.1875 to 0.1875
- norm_gain: float32 [1024], replicated, may hold values from 0.1 to 1.9
- w_hidden: bfloat16 [1024, 1024], P(None, 'mp'), may hold values from -0.1875 to 0.1875
- action_embed: bfloat16 [18, 1024], P(None, 'mp'), may hold values from -6 to 6
- w_out: bfloat16 [1024, 1024], P('mp'), may hold values from -0.1875 to 0.1875
Outputs:
- predicted: bfloat16 [8, 8, 128, 4, 1024], P('rep', None, 'tm', None, 'mp'), parts along dimension 0
The draws below stay inside these ranges and needn't reach their ends.
There are 2 independent parts, one for each index of `rep`. The reference program is written for one: setup_inputs(seed, part) draws one part's arguments, and reference() takes and returns one part's arrays. A program takes and returns all parts, laid end to end along the dimension named above; an argument that names none is the same for every part. Nothing has to cross between parts.
All inputs are finite; a program needn't handle non-finite values. No bound on the sum of `resets` on one device may be relied on, other than what follows from the above.
Results may differ from the reference program's by a relative error of at most 0.015.
Values may be sent and summed in bfloat16 or wider, within the bound.
No kernel may reach another device: no remote copies, remote signals or barrier semaphores. Data moves between devices by JAX's collectives and lax.ppermute only.
A program may use at most 64 MiB of HBM per device.

```python
import jax
import jax.numpy as jnp
from jax import lax

H = 1024
P_SIZE = 1024
FFH = 1024
ACTIONS = 18
IMAG = 4
BATCH = 4
STEP_DEV = 128
LEN = 1024
BLOCKS = 8
N_MP = 2


def draw_decay_rates(key, part):
    lower = 0.25 / LEN
    upper = 0.03
    spread = jax.random.uniform(key, (P_SIZE,), jnp.float32)
    return jnp.exp(jnp.log(lower) + spread * (jnp.log(upper) - jnp.log(lower)))


def touch_ends(values, key, smallest, top_value):
    index_at = [jax.random.randint(jax.random.fold_in(key, axis), (), 0, length) for axis, length in enumerate(values.shape)]
    main_axis = values.shape.index(max(values.shape))
    next_to = index_at[:main_axis] + [(index_at[main_axis] + 1) % values.shape[main_axis]] + index_at[main_axis + 1:]
    return values.at[tuple(index_at)].set(smallest).at[tuple(next_to)].set(top_value)


def steps_of(rng, shape, split, smallest, high):
    factor_of, own = 1.0, jax.random.fold_in(rng, 6)
    for dim, blocks in split:
        heights = jnp.exp(jax.random.uniform(jax.random.fold_in(own, dim), (blocks,), jnp.float32, smallest / len(split), high / len(split)))
        factor_of = factor_of * jnp.repeat(heights, shape[dim] // blocks).reshape([-1 if axis == dim else 1 for axis in range(len(shape))])
    return factor_of


def scatter_about(rng, extent, scale, reach, shards=(), kind=jnp.bfloat16):
    values = jax.random.normal(rng, extent, jnp.float32) * scale
    if len(shards) > 0:
        values = steps_of(rng, extent, shards, -0.22, 0.18) * values
    return jnp.clip(values, min=-reach, max=reach).astype(kind)


def setup_inputs(seed: int = 0, part: int = 0) -> dict:
    splits = jax.random.split(jax.random.key(seed), 11)
    part_keys = jax.random.split(jax.random.fold_in(splits[10], part), 11)
    return {
        "inputs": scatter_about(part_keys[0], (BATCH, LEN, H), 1.0, 6.0, ((1, 8),)),
        "resets": touch_ends((jax.random.randint(part_keys[1], (BATCH, LEN), 0, 1024) < 1).astype(jnp.int32), jax.random.fold_in(part_keys[1], 1), 0, 1),
        "actions": touch_ends(jax.random.randint(part_keys[2], (BATCH, BLOCKS, STEP_DEV, IMAG), 0, ACTIONS), jax.random.fold_in(part_keys[2], 1), 0, ACTIONS - 1).astype(jnp.int32),
        "in_proj": scatter_about(splits[3], (H, P_SIZE), H ** -0.5, 0.1875, ((1, 2),)),
        "decay_rates": draw_decay_rates(jax.random.fold_in(splits[10], 71), part),
        "readout_w": scatter_about(splits[5], (P_SIZE, H), P_SIZE ** -0.5, 0.1875, ((0, 2),)),
        "norm_gain": jnp.clip(1.0 + 0.18 * jax.random.normal(splits[6], (H,), jnp.float32), 0.1, 1.9),
        "w_hidden": scatter_about(splits[7], (H, FFH), H ** -0.5, 0.1875, ((1, 2),)),
        "action_embed": scatter_about(splits[8], (ACTIONS, FFH), 1.0, 6.0, ((1, 2),)),
        "w_out": scatter_about(splits[9], (FFH, H), FFH ** -0.5, 0.1875, ((0, 2),)),
    }


def imagine_rows(current, chosen, decays, scaling, in_proj, readout_w, norm_gain, w_hidden, action_embed, w_out):
    width_part = current.shape[1] // N_MP
    table_ids = jnp.arange(action_embed.shape[0], dtype=jnp.int32)
    outputs = []
    for step in range(IMAG):
        rounded_state = current.astype(jnp.bfloat16)
        features = jnp.zeros((current.shape[0], readout_w.shape[1]), jnp.float32)
        for block in range(N_MP):
            partial_sum = jnp.dot(rounded_state[:, block * width_part:(block + 1) * width_part], readout_w[block * width_part:(block + 1) * width_part], preferred_element_type=jnp.float32)
            features = features + lax.optimization_barrier(partial_sum.astype(jnp.bfloat16)).astype(jnp.float32)
        mean_sq = lax.optimization_barrier(jnp.mean(features * features, axis=-1, keepdims=True))
        normed = (features * lax.rsqrt(mean_sq + 1e-06) * norm_gain).astype(jnp.bfloat16)
        one_hot = (chosen[:, step][:, None] == table_ids[None, :]).astype(jnp.bfloat16)
        pre_act = jnp.dot(normed, w_hidden, preferred_element_type=jnp.float32) + jnp.dot(one_hot, action_embed, preferred_element_type=jnp.float32)
        hidden = jax.nn.silu(pre_act).astype(jnp.bfloat16)
        guessed = jnp.dot(hidden, w_out, preferred_element_type=jnp.float32).astype(jnp.bfloat16)
        outputs.append(guessed)
        if step < IMAG - 1:
            current = decays * current + scaling * jnp.dot(guessed, in_proj, preferred_element_type=jnp.float32)
    return jnp.stack(outputs, axis=1)

def reference(inputs, resets, actions, in_proj, decay_rates, readout_w, norm_gain, w_hidden, action_embed, w_out):
    decays = jnp.exp(-decay_rates)
    scaling = jnp.sqrt(1.0 - decays * decays)
    batch, length, width = inputs.shape
    driven = jnp.dot(inputs.reshape(batch * length, width), in_proj, preferred_element_type=jnp.float32).reshape(batch, length, -1) * scaling
    keep_mask = (1 - resets).astype(jnp.float32)

    def advance(current, pieces):
        drive_now, keep_now = pieces
        current = keep_now[:, None] * decays * current + drive_now
        return (current, current)
    start = jnp.zeros((batch, decay_rates.shape[0]), jnp.float32)
    final_state, states = lax.scan(advance, start, (jnp.swapaxes(driven, 0, 1), jnp.swapaxes(keep_mask, 0, 1)))
    posterior = jnp.swapaxes(states, 0, 1)
    flat_actions = actions.reshape(batch, length, actions.shape[3])

    def one_sequence(pair):
        return imagine_rows(pair[0], pair[1], decays, scaling, in_proj, readout_w, norm_gain, w_hidden, action_embed, w_out)
    result = lax.map(one_sequence, (posterior, flat_actions))
    return result.reshape(batch, actions.shape[1], actions.shape[2], IMAG, result.shape[-1])
```

```python
import jax
import jax.numpy as jnp
from jax import lax
from jax.experimental import pallas as pl
from jax.experimental.pallas import tpu as pltpu
from jax.sharding import PartitionSpec as P


def _scan_kernel(x_ref, g_ref, o_ref):
    nb, steps, width = x_ref.shape

    def body(t, states):
        row = pl.ds(t, 1)
        new = []
        for b in range(nb):
            h = g_ref[b, row, :] * states[b] + x_ref[b, row, :]
            o_ref[b, row, :] = h
            new.append(h)
        return tuple(new)

    start = tuple(jnp.zeros((1, width), jnp.float32) for _ in range(nb))
    lax.fori_loop(0, steps, body, start, unroll=8)


def local_scan(driven, gates):
    size = driven.size
    return pl.pallas_call(
        _scan_kernel,
        out_shape=jax.ShapeDtypeStruct(driven.shape, jnp.float32),
        in_specs=[pl.BlockSpec(memory_space=pltpu.VMEM)] * 2,
        out_specs=pl.BlockSpec(memory_space=pltpu.VMEM),
        cost_estimate=pl.CostEstimate(flops=2 * size, bytes_accessed=12 * size, transcendentals=0),
    )(driven, gates)


def per_device(
    inputs,
    resets,
    actions,
    in_proj,
    decay_rates,
    readout_w,
    norm_gain,
    w_hidden,
    action_embed,
    w_out,
):
    m = lax.axis_index("mp")
    d = lax.axis_index("tm")
    ntm = lax.axis_size("tm")
    swap = [(0, 1), (1, 0)]

    def partner(x):
        return lax.ppermute(x, "mp", swap)

    half = in_proj.shape[1]
    ip_o = partner(in_proj)
    r_o = partner(readout_w)
    wh_o = partner(w_hidden)
    wo_o = partner(w_out)
    emb_o = partner(action_embed)
    ip = jnp.concatenate([in_proj, ip_o], axis=1)
    wh = jnp.concatenate([w_hidden, wh_o], axis=1)
    wo = jnp.concatenate([w_out, wo_o], axis=0)
    emb = jnp.concatenate([action_embed, emb_o], axis=1)

    rates = jnp.concatenate(
        [
            lax.dynamic_slice_in_dim(decay_rates, m * half, half),
            lax.dynamic_slice_in_dim(decay_rates, (1 - m) * half, half),
        ]
    )
    decays = jnp.exp(-rates)
    scaling = jnp.sqrt(1.0 - decays * decays)
    width = decays.shape[0]

    seqs, steps, feat = inputs.shape
    bh = seqs // 2
    x = lax.dynamic_slice_in_dim(inputs, m * bh, bh, 0)
    driven = (
        jnp.dot(x.reshape(bh * steps, feat), ip, preferred_element_type=jnp.float32).reshape(
            bh, steps, width
        )
        * scaling
    )
    my_resets = lax.dynamic_slice_in_dim(resets, m * bh, bh, 0)
    keep = (1 - my_resets).astype(jnp.float32)
    gates = keep[:, :, None] * decays
    local = local_scan(driven, gates)

    positions = lax.broadcasted_iota(jnp.int32, my_resets.shape, 1)
    first = jnp.min(jnp.where(my_resets != 0, positions, steps), axis=1).astype(jnp.float32)
    payload = jnp.concatenate(
        [local[:, -1, :], jnp.broadcast_to(first[:, None], (bh, 128))], axis=1
    )
    gathered = lax.all_gather(payload, "tm")
    ends = gathered[:, :, :width]
    firsts = gathered[:, :, width]

    sub = steps // ntm
    send = local.astype(jnp.bfloat16).reshape(bh, ntm, sub, width)
    recv = lax.all_to_all(send, "tm", split_axis=1, concat_axis=1, tiled=True)

    nblocks = gathered.shape[0]
    whole_block = decays ** steps
    gain = jnp.where(firsts >= steps, 1.0, 0.0)[:, :, None] * whole_block
    total = ends
    offset = 1
    while offset < nblocks:
        gain_prev = jnp.concatenate([jnp.ones_like(gain[:offset]), gain[:-offset]], axis=0)
        total_prev = jnp.concatenate([jnp.zeros_like(total[:offset]), total[:-offset]], axis=0)
        total = gain * total_prev + total
        gain = gain * gain_prev
        offset *= 2
    carry = jnp.concatenate([jnp.zeros_like(total[:1]), total[:-1]], axis=0)

    t_glob = d * sub + lax.broadcasted_iota(jnp.int32, (sub,), 0)
    powers = decays[None, :] ** (t_glob[:, None] + 1).astype(jnp.float32)
    alive = t_glob[None, None, :].astype(jnp.float32) < jnp.swapaxes(firsts, 0, 1)[:, :, None]
    cum = jnp.where(alive[..., None], powers[None, None], 0.0)
    posterior = recv.astype(jnp.float32) + cum * jnp.swapaxes(carry, 0, 1)[:, :, None, :]

    _, blocks, _, horizon = actions.shape
    rows = bh * blocks * sub
    current = posterior.reshape(rows, width)
    my_actions = lax.dynamic_slice_in_dim(actions, m * bh, bh, 0).reshape(rows, horizon)
    table_ids = jnp.arange(emb.shape[0], dtype=jnp.int32)
    kept, given = [], []
    for step in range(horizon):
        rounded = current.astype(jnp.bfloat16)
        features = jnp.dot(
            rounded[:, :half], readout_w, preferred_element_type=jnp.float32
        ).astype(jnp.bfloat16).astype(jnp.float32) + jnp.dot(
            rounded[:, half:], r_o, preferred_element_type=jnp.float32
        ).astype(jnp.bfloat16).astype(jnp.float32)
        mean_sq = jnp.mean(features * features, axis=-1, keepdims=True)
        normed = (features * lax.rsqrt(mean_sq + 1e-06) * norm_gain).astype(jnp.bfloat16)
        one_hot = (my_actions[:, step][:, None] == table_ids[None, :]).astype(jnp.bfloat16)
        pre_act = jnp.dot(normed, wh, preferred_element_type=jnp.float32) + jnp.dot(
            one_hot, emb, preferred_element_type=jnp.float32
        )
        hidden = jax.nn.silu(pre_act).astype(jnp.bfloat16)
        guessed = jnp.dot(hidden, wo, preferred_element_type=jnp.float32).astype(jnp.bfloat16)
        kept.append(lax.dynamic_slice_in_dim(guessed, m * half, half, 1))
        given.append(partner(lax.dynamic_slice_in_dim(guessed, (1 - m) * half, half, 1)))
        if step < horizon - 1:
            current = decays * current + scaling * jnp.dot(
                guessed, ip, preferred_element_type=jnp.float32
            )
    mine = jnp.stack(kept, axis=1).reshape(bh, blocks, sub, horizon, half)
    theirs = jnp.stack(given, axis=1).reshape(bh, blocks, sub, horizon, half)
    first_half = jnp.where(m == 0, mine, theirs)
    second_half = jnp.where(m == 0, theirs, mine)
    return jnp.concatenate([first_half, second_half], axis=0)


def solution(mesh):
    in_specs = (
        P("rep", "tm", None),
        P("rep", "tm"),
        P("rep", None, "tm", None),
        P(None, "mp"),
        P(),
        P("mp", None),
        P(),
        P(None, "mp"),
        P(None, "mp"),
        P("mp", None),
    )
    out_specs = P("rep", None, "tm", None, "mp")
    return jax.shard_map(
        per_device, mesh=mesh, in_specs=in_specs, out_specs=out_specs, check_vma=False
    )
```

```python
import jax
import jax.numpy as jnp
from jax import lax
from jax.experimental import pallas as pl
from jax.experimental.pallas import tpu as pltpu
from jax.sharding import PartitionSpec as P


def _scan_kernel(x_ref, g_ref, o_ref):
    nb, steps, width = x_ref.shape

    def body(t, states):
        row = pl.ds(t, 1)
        new = []
        for b in range(nb):
            h = g_ref[b, row, :] * states[b] + x_ref[b, row, :]
            o_ref[b, row, :] = h
            new.append(h)
        return tuple(new)

    start = tuple(jnp.zeros((1, width), jnp.float32) for _ in range(nb))
    lax.fori_loop(0, steps, body, start, unroll=8)


def local_scan(driven, gates):
    size = driven.size
    return pl.pallas_call(
        _scan_kernel,
        out_shape=jax.ShapeDtypeStruct(driven.shape, jnp.float32),
        in_specs=[pl.BlockSpec(memory_space=pltpu.VMEM)] * 2,
        out_specs=pl.BlockSpec(memory_space=pltpu.VMEM),
        cost_estimate=pl.CostEstimate(flops=2 * size, bytes_accessed=12 * size, transcendentals=0),
    )(driven, gates)


def gather_blocks(value, axis, mine, count):
    if count & (count - 1):
        return lax.all_gather(value, axis)
    held = value[None]
    shift = 1
    while shift < count:
        pairs = [(i, (i + shift) % count) for i in range(count)]
        held = jnp.concatenate([held, lax.ppermute(held, axis, pairs)], axis=0)
        shift *= 2
    order = (mine - jnp.arange(count, dtype=jnp.int32)) % count
    return jnp.take(held, order, axis=0)


def per_device(
    inputs,
    resets,
    actions,
    in_proj,
    decay_rates,
    readout_w,
    norm_gain,
    w_hidden,
    action_embed,
    w_out,
):
    m = lax.axis_index("mp")
    d = lax.axis_index("tm")
    ntm = lax.axis_size("tm")
    swap = [(0, 1), (1, 0)]

    def partner(x):
        return lax.ppermute(x, "mp", swap)

    half = in_proj.shape[1]
    ip_o = partner(in_proj)
    r_o = partner(readout_w)
    wh_o = partner(w_hidden)
    wo_o = partner(w_out)
    emb_o = partner(action_embed)
    ip = jnp.concatenate([in_proj, ip_o], axis=1)
    wh = jnp.concatenate([w_hidden, wh_o], axis=1)
    wo = jnp.concatenate([w_out, wo_o], axis=0)
    emb = jnp.concatenate([action_embed, emb_o], axis=1)

    rates = jnp.concatenate(
        [
            lax.dynamic_slice_in_dim(decay_rates, m * half, half),
            lax.dynamic_slice_in_dim(decay_rates, (1 - m) * half, half),
        ]
    )
    decays = jnp.exp(-rates)
    scaling = jnp.sqrt(1.0 - decays * decays)
    width = decays.shape[0]

    seqs, steps, feat = inputs.shape
    bh = seqs // 2
    x = lax.dynamic_slice_in_dim(inputs, m * bh, bh, 0)
    driven = (
        jnp.dot(x.reshape(bh * steps, feat), ip, preferred_element_type=jnp.float32).reshape(
            bh, steps, width
        )
        * scaling
    )
    my_resets = lax.dynamic_slice_in_dim(resets, m * bh, bh, 0)
    keep = (1 - my_resets).astype(jnp.float32)
    gates = keep[:, :, None] * decays
    local = local_scan(driven, gates)

    positions = lax.broadcasted_iota(jnp.int32, my_resets.shape, 1)
    first = jnp.min(jnp.where(my_resets != 0, positions, steps), axis=1).astype(jnp.float32)
    payload = jnp.concatenate(
        [local[:, -1, :], jnp.broadcast_to(first[:, None], (bh, 128))], axis=1
    )
    gathered = gather_blocks(payload, "tm", d, ntm)
    ends = gathered[:, :, :width]
    firsts = gathered[:, :, width]

    sub = steps // ntm
    send = local.astype(jnp.bfloat16).reshape(bh, ntm, sub, width)
    recv = lax.all_to_all(send, "tm", split_axis=1, concat_axis=1, tiled=True)

    nblocks = gathered.shape[0]
    whole_block = decays ** steps
    gain = jnp.where(firsts >= steps, 1.0, 0.0)[:, :, None] * whole_block
    total = ends
    offset = 1
    while offset < nblocks:
        gain_prev = jnp.concatenate([jnp.ones_like(gain[:offset]), gain[:-offset]], axis=0)
        total_prev = jnp.concatenate([jnp.zeros_like(total[:offset]), total[:-offset]], axis=0)
        total = gain * total_prev + total
        gain = gain * gain_prev
        offset *= 2
    carry = jnp.concatenate([jnp.zeros_like(total[:1]), total[:-1]], axis=0)

    t_glob = d * sub + lax.broadcasted_iota(jnp.int32, (sub,), 0)
    powers = decays[None, :] ** (t_glob[:, None] + 1).astype(jnp.float32)
    alive = t_glob[None, None, :].astype(jnp.float32) < jnp.swapaxes(firsts, 0, 1)[:, :, None]
    cum = jnp.where(alive[..., None], powers[None, None], 0.0)
    posterior = recv.astype(jnp.float32) + cum * jnp.swapaxes(carry, 0, 1)[:, :, None, :]

    _, blocks, _, horizon = actions.shape
    rows = bh * blocks * sub
    current = posterior.reshape(rows, width)
    my_actions = lax.dynamic_slice_in_dim(actions, m * bh, bh, 0).reshape(rows, horizon)
    table_ids = jnp.arange(emb.shape[0], dtype=jnp.int32)
    kept, given = [], []
    for step in range(horizon):
        rounded = current.astype(jnp.bfloat16)
        features = jnp.dot(
            rounded[:, :half], readout_w, preferred_element_type=jnp.float32
        ).astype(jnp.bfloat16).astype(jnp.float32) + jnp.dot(
            rounded[:, half:], r_o, preferred_element_type=jnp.float32
        ).astype(jnp.bfloat16).astype(jnp.float32)
        mean_sq = jnp.mean(features * features, axis=-1, keepdims=True)
        normed = (features * lax.rsqrt(mean_sq + 1e-06) * norm_gain).astype(jnp.bfloat16)
        one_hot = (my_actions[:, step][:, None] == table_ids[None, :]).astype(jnp.bfloat16)
        pre_act = jnp.dot(normed, wh, preferred_element_type=jnp.float32) + jnp.dot(
            one_hot, emb, preferred_element_type=jnp.float32
        )
        hidden = jax.nn.silu(pre_act).astype(jnp.bfloat16)
        guessed = jnp.dot(hidden, wo, preferred_element_type=jnp.float32).astype(jnp.bfloat16)
        kept.append(lax.dynamic_slice_in_dim(guessed, m * half, half, 1))
        given.append(partner(lax.dynamic_slice_in_dim(guessed, (1 - m) * half, half, 1)))
        if step < horizon - 1:
            current = decays * current + scaling * jnp.dot(
                guessed, ip, preferred_element_type=jnp.float32
            )
    mine = jnp.stack(kept, axis=1).reshape(bh, blocks, sub, horizon, half)
    theirs = jnp.stack(given, axis=1).reshape(bh, blocks, sub, horizon, half)
    first_half = jnp.where(m == 0, mine, theirs)
    second_half = jnp.where(m == 0, theirs, mine)
    return jnp.concatenate([first_half, second_half], axis=0)


def solution(mesh):
    in_specs = (
        P("rep", "tm", None),
        P("rep", "tm"),
        P("rep", None, "tm", None),
        P(None, "mp"),
        P(),
        P("mp", None),
        P(),
        P(None, "mp"),
        P(None, "mp"),
        P("mp", None),
    )
    out_specs = P("rep", None, "tm", None, "mp")
    return jax.shard_map(
        per_device, mesh=mesh, in_specs=in_specs, out_specs=out_specs, check_vma=False
    )
```

```python
import jax
import jax.numpy as jnp
from jax import lax
from jax.experimental import pallas as pl
from jax.experimental.pallas import tpu as pltpu
from jax.sharding import PartitionSpec as P


def _scan_kernel(x_ref, g_ref, o_ref):
    nb, steps, width = x_ref.shape

    def body(t, states):
        row = pl.ds(t, 1)
        new = []
        for b in range(nb):
            h = g_ref[b, row, :] * states[b] + x_ref[b, row, :]
            o_ref[b, row, :] = h
            new.append(h)
        return tuple(new)

    start = tuple(jnp.zeros((1, width), jnp.float32) for _ in range(nb))
    lax.fori_loop(0, steps, body, start, unroll=8)


def local_scan(driven, gates):
    size = driven.size
    return pl.pallas_call(
        _scan_kernel,
        out_shape=jax.ShapeDtypeStruct(driven.shape, jnp.float32),
        in_specs=[pl.BlockSpec(memory_space=pltpu.VMEM)] * 2,
        out_specs=pl.BlockSpec(memory_space=pltpu.VMEM),
        cost_estimate=pl.CostEstimate(flops=2 * size, bytes_accessed=12 * size, transcendentals=0),
    )(driven, gates)


def gather_blocks(value, axis, mine, count):
    if count & (count - 1):
        return lax.all_gather(value, axis)
    held = value[None]
    shift = 1
    while shift < count:
        pairs = [(i, (i + shift) % count) for i in range(count)]
        held = jnp.concatenate([held, lax.ppermute(held, axis, pairs)], axis=0)
        shift *= 2
    order = (mine - jnp.arange(count, dtype=jnp.int32)) % count
    return jnp.take(held, order, axis=0)


def per_device(
    inputs,
    resets,
    actions,
    in_proj,
    decay_rates,
    readout_w,
    norm_gain,
    w_hidden,
    action_embed,
    w_out,
):
    m = lax.axis_index("mp")
    d = lax.axis_index("tm")
    ntm = lax.axis_size("tm")
    swap = [(0, 1), (1, 0)]

    def partner(x):
        return lax.ppermute(x, "mp", swap)

    half = in_proj.shape[1]
    ip_o = partner(in_proj)
    r_o = partner(readout_w)
    wh_o = partner(w_hidden)
    wo_o = partner(w_out)
    emb_o = partner(action_embed)
    ip = jnp.concatenate([in_proj, ip_o], axis=1)

    rates = jnp.concatenate(
        [
            lax.dynamic_slice_in_dim(decay_rates, m * half, half),
            lax.dynamic_slice_in_dim(decay_rates, (1 - m) * half, half),
        ]
    )
    decays = jnp.exp(-rates)
    scaling = jnp.sqrt(1.0 - decays * decays)
    width = decays.shape[0]

    seqs, steps, feat = inputs.shape
    bh = seqs // 2
    x = lax.dynamic_slice_in_dim(inputs, m * bh, bh, 0)
    driven = (
        jnp.dot(x.reshape(bh * steps, feat), ip, preferred_element_type=jnp.float32).reshape(
            bh, steps, width
        )
        * scaling
    )
    my_resets = lax.dynamic_slice_in_dim(resets, m * bh, bh, 0)
    keep = (1 - my_resets).astype(jnp.float32)
    gates = keep[:, :, None] * decays
    local = local_scan(driven, gates)

    positions = lax.broadcasted_iota(jnp.int32, my_resets.shape, 1)
    first = jnp.min(jnp.where(my_resets != 0, positions, steps), axis=1).astype(jnp.float32)
    payload = jnp.concatenate(
        [local[:, -1, :], jnp.broadcast_to(first[:, None], (bh, 128))], axis=1
    )
    gathered = gather_blocks(payload, "tm", d, ntm)
    ends = gathered[:, :, :width]
    firsts = gathered[:, :, width]

    sub = steps // ntm
    send = local.astype(jnp.bfloat16).reshape(bh, ntm, sub, width)
    recv = lax.all_to_all(send, "tm", split_axis=1, concat_axis=1, tiled=True)

    nblocks = gathered.shape[0]
    whole_block = decays ** steps
    gain = jnp.where(firsts >= steps, 1.0, 0.0)[:, :, None] * whole_block
    total = ends
    offset = 1
    while offset < nblocks:
        gain_prev = jnp.concatenate([jnp.ones_like(gain[:offset]), gain[:-offset]], axis=0)
        total_prev = jnp.concatenate([jnp.zeros_like(total[:offset]), total[:-offset]], axis=0)
        total = gain * total_prev + total
        gain = gain * gain_prev
        offset *= 2
    carry = jnp.concatenate([jnp.zeros_like(total[:1]), total[:-1]], axis=0)

    t_glob = d * sub + lax.broadcasted_iota(jnp.int32, (sub,), 0)
    powers = decays[None, :] ** (t_glob[:, None] + 1).astype(jnp.float32)
    alive = t_glob[None, None, :].astype(jnp.float32) < jnp.swapaxes(firsts, 0, 1)[:, :, None]
    cum = jnp.where(alive[..., None], powers[None, None], 0.0)
    posterior = recv.astype(jnp.float32) + cum * jnp.swapaxes(carry, 0, 1)[:, :, None, :]

    _, blocks, _, horizon = actions.shape
    rows = bh * blocks * sub
    current = posterior.reshape(rows, width)
    my_actions = lax.dynamic_slice_in_dim(actions, m * bh, bh, 0).reshape(rows, horizon)
    table = jnp.concatenate([action_embed, emb_o], axis=1)
    table = jnp.pad(table, ((0, 128 - table.shape[0]), (0, 0)))
    one_hot = (
        jnp.swapaxes(my_actions, 0, 1)[:, :, None] == jnp.arange(128, dtype=jnp.int32)
    ).astype(jnp.bfloat16)
    vecs = jnp.stack([decays, scaling, norm_gain], axis=0)
    side = jnp.reshape(m, (1,)).astype(jnp.int32)
    keep_part, give_part = imagine(
        side, current, one_hot, vecs, readout_w, r_o, w_hidden, wh_o, table, w_out, wo_o,
        in_proj, ip_o,
    )
    got = partner(give_part)

    def arrange(part):
        return jnp.transpose(part.reshape(horizon, bh, blocks, sub, half), (1, 2, 3, 0, 4))

    mine, theirs = arrange(keep_part), arrange(got)
    first_half = jnp.where(m == 0, mine, theirs)
    second_half = jnp.where(m == 0, theirs, mine)
    return jnp.concatenate([first_half, second_half], axis=0)


def _imagine_kernel(
    side_ref, cur_ref, hot_ref, vec_ref, r_a, r_b, wh_a, wh_b, emb_ref, wo_a, wo_b, ip_a, ip_b,
    keep_ref, give_ref,
):
    horizon, rows, _ = hot_ref.shape
    half = r_a.shape[0]
    width = 2 * half
    tile = 128
    lead = side_ref[0] == 0

    def dot(a, b):
        return jnp.dot(a, b, preferred_element_type=jnp.float32)

    def chunk(c, carry):
        rs = pl.ds(pl.multiple_of(c * tile, tile), tile)
        cur_a = cur_ref[rs, :half]
        cur_b = cur_ref[rs, half:]
        for step in range(horizon):
            f = dot(cur_a.astype(jnp.bfloat16), r_a[...]).astype(jnp.bfloat16).astype(
                jnp.float32
            ) + dot(cur_b.astype(jnp.bfloat16), r_b[...]).astype(jnp.bfloat16).astype(jnp.float32)
            mean_sq = jnp.sum(f * f, axis=-1, keepdims=True) * (1.0 / width)
            normed = (f * lax.rsqrt(mean_sq + 1e-06) * vec_ref[2:3, :]).astype(jnp.bfloat16)
            hot = hot_ref[step, rs, :]
            pre_a = dot(normed, wh_a[...]) + dot(hot, emb_ref[:, :half])
            pre_b = dot(normed, wh_b[...]) + dot(hot, emb_ref[:, half:])
            hid_a = (pre_a * jax.nn.sigmoid(pre_a)).astype(jnp.bfloat16)
            hid_b = (pre_b * jax.nn.sigmoid(pre_b)).astype(jnp.bfloat16)
            lo = (dot(hid_a, wo_a[:, :half]) + dot(hid_b, wo_b[:, :half])).astype(jnp.bfloat16)
            hi = (dot(hid_a, wo_a[:, half:]) + dot(hid_b, wo_b[:, half:])).astype(jnp.bfloat16)
            keep_ref[step, rs, :] = jnp.where(lead, lo, hi)
            give_ref[step, rs, :] = jnp.where(lead, hi, lo)
            if step < horizon - 1:
                up_a = dot(lo, ip_a[:half, :]) + dot(hi, ip_a[half:, :])
                up_b = dot(lo, ip_b[:half, :]) + dot(hi, ip_b[half:, :])
                cur_a = vec_ref[0:1, :half] * cur_a + vec_ref[1:2, :half] * up_a
                cur_b = vec_ref[0:1, half:] * cur_b + vec_ref[1:2, half:] * up_b
        return carry

    lax.fori_loop(0, rows // tile, chunk, 0)


def imagine(side, current, one_hot, vecs, *weights):
    horizon, rows, _ = one_hot.shape
    half = weights[0].shape[0]
    out = jax.ShapeDtypeStruct((horizon, rows, half), jnp.bfloat16)
    vmem = pl.BlockSpec(memory_space=pltpu.VMEM)
    flops = 2 * rows * horizon * 4 * (2 * half) * (2 * half)
    return pl.pallas_call(
        _imagine_kernel,
        out_shape=(out, out),
        in_specs=[pl.BlockSpec(memory_space=pltpu.SMEM)] + [vmem] * (3 + len(weights)),
        out_specs=(vmem, vmem),
        compiler_params=pltpu.CompilerParams(vmem_limit_bytes=48 * 1024 * 1024),
        cost_estimate=pl.CostEstimate(
            flops=flops, bytes_accessed=16 * 1024 * 1024, transcendentals=rows * horizon * 2 * half
        ),
    )(side, current, one_hot, vecs, *weights)


def solution(mesh):
    in_specs = (
        P("rep", "tm", None),
        P("rep", "tm"),
        P("rep", None, "tm", None),
        P(None, "mp"),
        P(),
        P("mp", None),
        P(),
        P(None, "mp"),
        P(None, "mp"),
        P("mp", None),
    )
    out_specs = P("rep", None, "tm", None, "mp")
    return jax.shard_map(
        per_device, mesh=mesh, in_specs=in_specs, out_specs=out_specs, check_vma=False
    )
```

```python
import jax
import jax.numpy as jnp
from jax import lax
from jax.experimental import pallas as pl
from jax.experimental.pallas import tpu as pltpu
from jax.sharding import PartitionSpec as P


def _scan_kernel(x_ref, g_ref, o_ref):
    nb, steps, width = x_ref.shape

    def body(t, states):
        row = pl.ds(t, 1)
        new = []
        for b in range(nb):
            h = g_ref[b, row, :] * states[b] + x_ref[b, row, :]
            o_ref[b, row, :] = h
            new.append(h)
        return tuple(new)

    start = tuple(jnp.zeros((1, width), jnp.float32) for _ in range(nb))
    lax.fori_loop(0, steps, body, start, unroll=8)


def local_scan(driven, gates):
    size = driven.size
    return pl.pallas_call(
        _scan_kernel,
        out_shape=jax.ShapeDtypeStruct(driven.shape, jnp.float32),
        in_specs=[pl.BlockSpec(memory_space=pltpu.VMEM)] * 2,
        out_specs=pl.BlockSpec(memory_space=pltpu.VMEM),
        cost_estimate=pl.CostEstimate(flops=2 * size, bytes_accessed=12 * size, transcendentals=0),
    )(driven, gates)


def body(
    inputs,
    resets,
    actions,
    in_proj,
    decay_rates,
    readout_w,
    norm_gain,
    w_hidden,
    action_embed,
    w_out,
):
    m = lax.axis_index("mp")
    d = lax.axis_index("tm")
    ntm = lax.axis_size("tm")
    swap = [(0, 1), (1, 0)]

    def partner(x):
        return lax.ppermute(x, "mp", swap)

    half = in_proj.shape[1]
    ip_o = partner(in_proj)
    r_o = partner(readout_w)
    wh_o = partner(w_hidden)
    wo_o = partner(w_out)
    emb_o = partner(action_embed)
    ip = jnp.concatenate([in_proj, ip_o], axis=1)

    rates = jnp.concatenate(
        [
            lax.dynamic_slice_in_dim(decay_rates, m * half, half),
            lax.dynamic_slice_in_dim(decay_rates, (1 - m) * half, half),
        ]
    )
    decays = jnp.exp(-rates)
    scaling = jnp.sqrt(1.0 - decays * decays)
    width = decays.shape[0]

    seqs, steps, feat = inputs.shape
    bh = seqs // 2
    x = lax.dynamic_slice_in_dim(inputs, m * bh, bh, 0)
    driven = (
        jnp.dot(x.reshape(bh * steps, feat), ip, preferred_element_type=jnp.float32).reshape(
            bh, steps, width
        )
        * scaling
    )
    my_resets = lax.dynamic_slice_in_dim(resets, m * bh, bh, 0)
    keep = (1 - my_resets).astype(jnp.float32)
    gates = keep[:, :, None] * decays
    sub = steps // ntm
    locals_ = [local_scan(driven[b : b + 1], gates[b : b + 1])[0] for b in range(bh)]
    positions = lax.broadcasted_iota(jnp.int32, my_resets.shape, 1)
    first = jnp.min(jnp.where(my_resets != 0, positions, steps), axis=1).astype(jnp.float32)
    ends_local = jnp.stack([loc[-1, :] for loc in locals_], axis=0)
    ends_hi = ends_local.astype(jnp.bfloat16)
    ends_lo = (ends_local - ends_hi.astype(jnp.float32)).astype(jnp.bfloat16)
    first_rows = jnp.broadcast_to(first[:, None], (bh, width)).astype(jnp.bfloat16)
    extra = jnp.concatenate([ends_hi, ends_lo, first_rows], axis=0)
    pad_rows = -(-extra.shape[0] // 16) * 16
    extra = jnp.pad(extra, ((0, pad_rows - extra.shape[0]), (0, 0)))
    recvs = []
    for b in range(bh):
        send = locals_[b].astype(jnp.bfloat16).reshape(ntm, sub, width)
        if b == 0:
            send = jnp.concatenate(
                [send, jnp.broadcast_to(extra[None], (ntm,) + extra.shape)], axis=1
            )
        recvs.append(lax.all_to_all(send, "tm", split_axis=0, concat_axis=0, tiled=True))
    got_extra = recvs[0][:, sub:]
    recvs[0] = recvs[0][:, :sub]
    ends = got_extra[:, :bh].astype(jnp.float32) + got_extra[:, bh : 2 * bh].astype(jnp.float32)
    firsts = got_extra[:, 2 * bh : 3 * bh, 0].astype(jnp.float32)
    gathered = ends

    nblocks = gathered.shape[0]
    whole_block = decays ** steps
    gain = jnp.where(firsts >= steps, 1.0, 0.0)[:, :, None] * whole_block
    total = ends
    offset = 1
    while offset < nblocks:
        gain_prev = jnp.concatenate([jnp.ones_like(gain[:offset]), gain[:-offset]], axis=0)
        total_prev = jnp.concatenate([jnp.zeros_like(total[:offset]), total[:-offset]], axis=0)
        total = gain * total_prev + total
        gain = gain * gain_prev
        offset *= 2
    carry = jnp.concatenate([jnp.zeros_like(total[:1]), total[:-1]], axis=0)

    t_glob = d * sub + lax.broadcasted_iota(jnp.int32, (sub,), 0)
    powers = decays[None, :] ** (t_glob[:, None] + 1).astype(jnp.float32)

    _, blocks, _, horizon = actions.shape
    rows = blocks * sub
    my_actions = lax.dynamic_slice_in_dim(actions, m * bh, bh, 0)
    table = jnp.concatenate([action_embed, emb_o], axis=1)
    table = jnp.pad(table, ((0, 128 - table.shape[0]), (0, 0)))
    vecs = jnp.stack([decays, scaling, norm_gain], axis=0)
    side = jnp.reshape(m, (1,)).astype(jnp.int32)

    def arrange(part):
        return jnp.transpose(part.reshape(horizon, blocks, sub, half), (1, 2, 0, 3))

    mine, theirs = [], []
    for b in range(bh):
        alive = t_glob[None, :].astype(jnp.float32) < firsts[:, b][:, None]
        cum = jnp.where(alive[..., None], powers[None], 0.0)
        posterior = recvs[b].astype(jnp.float32) + cum * carry[:, b][:, None, :]
        current = posterior.reshape(rows, width)
        one_hot = (
            jnp.swapaxes(my_actions[b].reshape(rows, horizon), 0, 1)[:, :, None]
            == jnp.arange(128, dtype=jnp.int32)
        ).astype(jnp.bfloat16)
        keep_part, give_part = imagine(
            side, current, one_hot, vecs, readout_w, r_o, w_hidden, wh_o, table, w_out, wo_o,
            in_proj, ip_o,
        )
        mine.append(arrange(keep_part))
        theirs.append(arrange(partner(give_part)))
    mine = jnp.stack(mine, axis=0)
    theirs = jnp.stack(theirs, axis=0)
    first_half = jnp.where(m == 0, mine, theirs)
    second_half = jnp.where(m == 0, theirs, mine)
    return jnp.concatenate([first_half, second_half], axis=0)


def _imagine_kernel(
    side_ref, cur_ref, hot_ref, vec_ref, r_a, r_b, wh_a, wh_b, emb_ref, wo_a, wo_b, ip_a, ip_b,
    keep_ref, give_ref,
):
    horizon, rows, _ = hot_ref.shape
    half = r_a.shape[0]
    width = 2 * half
    tile = 128
    lead = side_ref[0] == 0

    def dot(a, b):
        return jnp.dot(a, b, preferred_element_type=jnp.float32)

    def chunk(c, carry):
        rs = pl.ds(pl.multiple_of(c * tile, tile), tile)
        cur_a = cur_ref[rs, :half]
        cur_b = cur_ref[rs, half:]
        for step in range(horizon):
            f = dot(cur_a.astype(jnp.bfloat16), r_a[...]).astype(jnp.bfloat16).astype(
                jnp.float32
            ) + dot(cur_b.astype(jnp.bfloat16), r_b[...]).astype(jnp.bfloat16).astype(jnp.float32)
            mean_sq = jnp.sum(f * f, axis=-1, keepdims=True) * (1.0 / width)
            normed = (f * lax.rsqrt(mean_sq + 1e-06) * vec_ref[2:3, :]).astype(jnp.bfloat16)
            hot = hot_ref[step, rs, :]
            pre_a = dot(normed, wh_a[...]) + dot(hot, emb_ref[:, :half])
            pre_b = dot(normed, wh_b[...]) + dot(hot, emb_ref[:, half:])
            hid_a = (pre_a * jax.nn.sigmoid(pre_a)).astype(jnp.bfloat16)
            hid_b = (pre_b * jax.nn.sigmoid(pre_b)).astype(jnp.bfloat16)
            lo = (dot(hid_a, wo_a[:, :half]) + dot(hid_b, wo_b[:, :half])).astype(jnp.bfloat16)
            hi = (dot(hid_a, wo_a[:, half:]) + dot(hid_b, wo_b[:, half:])).astype(jnp.bfloat16)
            keep_ref[step, rs, :] = jnp.where(lead, lo, hi)
            give_ref[step, rs, :] = jnp.where(lead, hi, lo)
            if step < horizon - 1:
                up_a = dot(lo, ip_a[:half, :]) + dot(hi, ip_a[half:, :])
                up_b = dot(lo, ip_b[:half, :]) + dot(hi, ip_b[half:, :])
                cur_a = vec_ref[0:1, :half] * cur_a + vec_ref[1:2, :half] * up_a
                cur_b = vec_ref[0:1, half:] * cur_b + vec_ref[1:2, half:] * up_b
        return carry

    lax.fori_loop(0, rows // tile, chunk, 0)


def imagine(side, current, one_hot, vecs, *weights):
    horizon, rows, _ = one_hot.shape
    half = weights[0].shape[0]
    out = jax.ShapeDtypeStruct((horizon, rows, half), jnp.bfloat16)
    vmem = pl.BlockSpec(memory_space=pltpu.VMEM)
    flops = 2 * rows * horizon * 4 * (2 * half) * (2 * half)
    return pl.pallas_call(
        _imagine_kernel,
        out_shape=(out, out),
        in_specs=[pl.BlockSpec(memory_space=pltpu.SMEM)] + [vmem] * (3 + len(weights)),
        out_specs=(vmem, vmem),
        compiler_params=pltpu.CompilerParams(vmem_limit_bytes=48 * 1024 * 1024),
        cost_estimate=pl.CostEstimate(
            flops=flops, bytes_accessed=16 * 1024 * 1024, transcendentals=rows * horizon * 2 * half
        ),
    )(side, current, one_hot, vecs, *weights)


def solution(mesh):
    in_specs = (
        P("rep", "tm", None),
        P("rep", "tm"),
        P("rep", None, "tm", None),
        P(None, "mp"),
        P(),
        P("mp", None),
        P(),
        P(None, "mp"),
        P(None, "mp"),
        P("mp", None),
    )
    out_specs = P("rep", None, "tm", None, "mp")
    return jax.shard_map(body, mesh=mesh, in_specs=in_specs, out_specs=out_specs, check_vma=False)
```

```python
import jax
import jax.numpy as jnp
from jax import lax
from jax.experimental import pallas as pl
from jax.experimental.pallas import tpu as pltpu
from jax.sharding import PartitionSpec as P


def _scan_kernel(x_ref, g_ref, o_ref):
    nb, steps, width = x_ref.shape

    def body(t, states):
        row = pl.ds(t, 1)
        new = []
        for b in range(nb):
            h = g_ref[b, row, :] * states[b] + x_ref[b, row, :]
            o_ref[b, row, :] = h
            new.append(h)
        return tuple(new)

    start = tuple(jnp.zeros((1, width), jnp.float32) for _ in range(nb))
    lax.fori_loop(0, steps, body, start, unroll=8)


def local_scan(driven, gates):
    size = driven.size
    return pl.pallas_call(
        _scan_kernel,
        out_shape=jax.ShapeDtypeStruct(driven.shape, jnp.float32),
        in_specs=[pl.BlockSpec(memory_space=pltpu.VMEM)] * 2,
        out_specs=pl.BlockSpec(memory_space=pltpu.VMEM),
        cost_estimate=pl.CostEstimate(flops=2 * size, bytes_accessed=12 * size, transcendentals=0),
    )(driven, gates)


def gather_blocks(value, axis, mine, count):
    if count & (count - 1):
        return lax.all_gather(value, axis)
    held = value[None]
    shift = 1
    while shift < count:
        pairs = [(i, (i + shift) % count) for i in range(count)]
        held = jnp.concatenate([held, lax.ppermute(held, axis, pairs)], axis=0)
        shift *= 2
    order = (mine - jnp.arange(count, dtype=jnp.int32)) % count
    return jnp.take(held, order, axis=0)


def per_device(
    inputs,
    resets,
    actions,
    in_proj,
    decay_rates,
    readout_w,
    norm_gain,
    w_hidden,
    action_embed,
    w_out,
):
    m = lax.axis_index("mp")
    d = lax.axis_index("tm")
    ntm = lax.axis_size("tm")
    swap = [(0, 1), (1, 0)]

    def partner(x):
        return lax.ppermute(x, "mp", swap)

    half = in_proj.shape[1]
    ip_o = partner(in_proj)
    r_o = partner(readout_w)
    wh_o = partner(w_hidden)
    wo_o = partner(w_out)
    emb_o = partner(action_embed)
    ip = jnp.concatenate([in_proj, ip_o], axis=1)

    rates = jnp.concatenate(
        [
            lax.dynamic_slice_in_dim(decay_rates, m * half, half),
            lax.dynamic_slice_in_dim(decay_rates, (1 - m) * half, half),
        ]
    )
    decays = jnp.exp(-rates)
    scaling = jnp.sqrt(1.0 - decays * decays)
    width = decays.shape[0]

    seqs, steps, feat = inputs.shape
    bh = seqs // 2
    x = lax.dynamic_slice_in_dim(inputs, m * bh, bh, 0)
    driven = (
        jnp.dot(x.reshape(bh * steps, feat), ip, preferred_element_type=jnp.float32).reshape(
            bh, steps, width
        )
        * scaling
    )
    my_resets = lax.dynamic_slice_in_dim(resets, m * bh, bh, 0)
    keep = (1 - my_resets).astype(jnp.float32)
    gates = keep[:, :, None] * decays
    local = local_scan(driven, gates)
    sub = steps // ntm

    positions = lax.broadcasted_iota(jnp.int32, my_resets.shape, 1)
    first = jnp.min(jnp.where(my_resets != 0, positions, steps), axis=1).astype(jnp.float32)
    ends_local = local[:, -1, :]
    ends_hi = ends_local.astype(jnp.bfloat16)
    ends_lo = (ends_local - ends_hi.astype(jnp.float32)).astype(jnp.bfloat16)
    first_rows = jnp.broadcast_to(first[:, None], (bh, width)).astype(jnp.bfloat16)
    extra = jnp.concatenate([ends_hi, ends_lo, first_rows], axis=0)
    pad_rows = -(-(extra.shape[0] + bh * sub) // 16) * 16 - bh * sub
    extra = jnp.pad(extra, ((0, pad_rows - extra.shape[0]), (0, 0)))
    states = jnp.swapaxes(local.astype(jnp.bfloat16).reshape(bh, ntm, sub, width), 0, 1)
    send = jnp.concatenate(
        [states.reshape(ntm, bh * sub, width), jnp.broadcast_to(extra[None], (ntm,) + extra.shape)],
        axis=1,
    )
    got = lax.all_to_all(send, "tm", split_axis=0, concat_axis=0, tiled=True)
    recv = jnp.swapaxes(got[:, : bh * sub].reshape(ntm, bh, sub, width), 0, 1)
    got_extra = got[:, bh * sub :]
    gathered = got_extra[:, :bh].astype(jnp.float32) + got_extra[:, bh : 2 * bh].astype(
        jnp.float32
    )
    ends = gathered
    firsts = got_extra[:, 2 * bh : 3 * bh, 0].astype(jnp.float32)

    nblocks = gathered.shape[0]
    whole_block = decays ** steps
    gain = jnp.where(firsts >= steps, 1.0, 0.0)[:, :, None] * whole_block
    total = ends
    offset = 1
    while offset < nblocks:
        gain_prev = jnp.concatenate([jnp.ones_like(gain[:offset]), gain[:-offset]], axis=0)
        total_prev = jnp.concatenate([jnp.zeros_like(total[:offset]), total[:-offset]], axis=0)
        total = gain * total_prev + total
        gain = gain * gain_prev
        offset *= 2
    carry = jnp.concatenate([jnp.zeros_like(total[:1]), total[:-1]], axis=0)

    t_glob = d * sub + lax.broadcasted_iota(jnp.int32, (sub,), 0)
    powers = decays[None, :] ** (t_glob[:, None] + 1).astype(jnp.float32)
    alive = t_glob[None, None, :].astype(jnp.float32) < jnp.swapaxes(firsts, 0, 1)[:, :, None]
    cum = jnp.where(alive[..., None], powers[None, None], 0.0)
    posterior = recv.astype(jnp.float32) + cum * jnp.swapaxes(carry, 0, 1)[:, :, None, :]

    _, blocks, _, horizon = actions.shape
    rows = bh * blocks * sub
    current = posterior.reshape(rows, width)
    my_actions = lax.dynamic_slice_in_dim(actions, m * bh, bh, 0).reshape(rows, horizon)
    table = jnp.concatenate([action_embed, emb_o], axis=1)
    table = jnp.pad(table, ((0, 128 - table.shape[0]), (0, 0)))
    one_hot = (
        jnp.swapaxes(my_actions, 0, 1)[:, :, None] == jnp.arange(128, dtype=jnp.int32)
    ).astype(jnp.bfloat16)
    vecs = jnp.stack([decays, scaling, norm_gain], axis=0)
    side = jnp.reshape(m, (1,)).astype(jnp.int32)
    keep_part, give_part = imagine(
        side, current, one_hot, vecs, readout_w, r_o, w_hidden, wh_o, table, w_out, wo_o,
        in_proj, ip_o,
    )
    got = partner(give_part)

    def arrange(part):
        return jnp.transpose(part.reshape(horizon, bh, blocks, sub, half), (1, 2, 3, 0, 4))

    mine, theirs = arrange(keep_part), arrange(got)
    first_half = jnp.where(m == 0, mine, theirs)
    second_half = jnp.where(m == 0, theirs, mine)
    return jnp.concatenate([first_half, second_half], axis=0)


def _imagine_kernel(
    side_ref, cur_ref, hot_ref, vec_ref, r_a, r_b, wh_a, wh_b, emb_ref, wo_a, wo_b, ip_a, ip_b,
    keep_ref, give_ref,
):
    horizon, rows, _ = hot_ref.shape
    half = r_a.shape[0]
    width = 2 * half
    tile = 128
    lead = side_ref[0] == 0

    def dot(a, b):
        return jnp.dot(a, b, preferred_element_type=jnp.float32)

    def chunk(c, carry):
        rs = pl.ds(pl.multiple_of(c * tile, tile), tile)
        cur_a = cur_ref[rs, :half]
        cur_b = cur_ref[rs, half:]
        for step in range(horizon):
            f = dot(cur_a.astype(jnp.bfloat16), r_a[...]).astype(jnp.bfloat16).astype(
                jnp.float32
            ) + dot(cur_b.astype(jnp.bfloat16), r_b[...]).astype(jnp.bfloat16).astype(jnp.float32)
            mean_sq = jnp.sum(f * f, axis=-1, keepdims=True) * (1.0 / width)
            normed = (f * lax.rsqrt(mean_sq + 1e-06) * vec_ref[2:3, :]).astype(jnp.bfloat16)
            hot = hot_ref[step, rs, :]
            pre_a = dot(normed, wh_a[...]) + dot(hot, emb_ref[:, :half])
            pre_b = dot(normed, wh_b[...]) + dot(hot, emb_ref[:, half:])
            hid_a = (pre_a * jax.nn.sigmoid(pre_a)).astype(jnp.bfloat16)
            hid_b = (pre_b * jax.nn.sigmoid(pre_b)).astype(jnp.bfloat16)
            lo = (dot(hid_a, wo_a[:, :half]) + dot(hid_b, wo_b[:, :half])).astype(jnp.bfloat16)
            hi = (dot(hid_a, wo_a[:, half:]) + dot(hid_b, wo_b[:, half:])).astype(jnp.bfloat16)
            keep_ref[step, rs, :] = jnp.where(lead, lo, hi)
            give_ref[step, rs, :] = jnp.where(lead, hi, lo)
            if step < horizon - 1:
                up_a = dot(lo, ip_a[:half, :]) + dot(hi, ip_a[half:, :])
                up_b = dot(lo, ip_b[:half, :]) + dot(hi, ip_b[half:, :])
                cur_a = vec_ref[0:1, :half] * cur_a + vec_ref[1:2, :half] * up_a
                cur_b = vec_ref[0:1, half:] * cur_b + vec_ref[1:2, half:] * up_b
        return carry

    lax.fori_loop(0, rows // tile, chunk, 0)


def imagine(side, current, one_hot, vecs, *weights):
    horizon, rows, _ = one_hot.shape
    half = weights[0].shape[0]
    out = jax.ShapeDtypeStruct((horizon, rows, half), jnp.bfloat16)
    vmem = pl.BlockSpec(memory_space=pltpu.VMEM)
    flops = 2 * rows * horizon * 4 * (2 * half) * (2 * half)
    return pl.pallas_call(
        _imagine_kernel,
        out_shape=(out, out),
        in_specs=[pl.BlockSpec(memory_space=pltpu.SMEM)] + [vmem] * (3 + len(weights)),
        out_specs=(vmem, vmem),
        compiler_params=pltpu.CompilerParams(vmem_limit_bytes=48 * 1024 * 1024),
        cost_estimate=pl.CostEstimate(
            flops=flops, bytes_accessed=16 * 1024 * 1024, transcendentals=rows * horizon * 2 * half
        ),
    )(side, current, one_hot, vecs, *weights)


def solution(mesh):
    in_specs = (
        P("rep", "tm", None),
        P("rep", "tm"),
        P("rep", None, "tm", None),
        P(None, "mp"),
        P(),
        P("mp", None),
        P(),
        P(None, "mp"),
        P(None, "mp"),
        P("mp", None),
    )
    out_specs = P("rep", None, "tm", None, "mp")
    return jax.shard_map(
        per_device, mesh=mesh, in_specs=in_specs, out_specs=out_specs, check_vma=False
    )
```

```python
import jax
import jax.numpy as jnp
from jax import lax
from jax.experimental import pallas as pl
from jax.experimental.pallas import tpu as pltpu
from jax.sharding import PartitionSpec as P


def _scan_kernel(x_ref, g_ref, o_ref):
    nb, steps, width = x_ref.shape

    def body(t, states):
        row = pl.ds(t, 1)
        new = []
        for b in range(nb):
            h = g_ref[b, row, :] * states[b] + x_ref[b, row, :]
            o_ref[b, row, :] = h
            new.append(h)
        return tuple(new)

    start = tuple(jnp.zeros((1, width), jnp.float32) for _ in range(nb))
    lax.fori_loop(0, steps, body, start, unroll=8)


def local_scan(driven, gates):
    size = driven.size
    return pl.pallas_call(
        _scan_kernel,
        out_shape=jax.ShapeDtypeStruct(driven.shape, jnp.float32),
        in_specs=[pl.BlockSpec(memory_space=pltpu.VMEM)] * 2,
        out_specs=pl.BlockSpec(memory_space=pltpu.VMEM),
        cost_estimate=pl.CostEstimate(flops=2 * size, bytes_accessed=12 * size, transcendentals=0),
    )(driven, gates)


def gather_blocks(value, axis, mine, count):
    if count & (count - 1):
        return lax.all_gather(value, axis)
    held = value[None]
    shift = 1
    while shift < count:
        pairs = [(i, (i + shift) % count) for i in range(count)]
        held = jnp.concatenate([held, lax.ppermute(held, axis, pairs)], axis=0)
        shift *= 2
    order = (mine - jnp.arange(count, dtype=jnp.int32)) % count
    return jnp.take(held, order, axis=0)


def per_device(
    inputs,
    resets,
    actions,
    in_proj,
    decay_rates,
    readout_w,
    norm_gain,
    w_hidden,
    action_embed,
    w_out,
):
    m = lax.axis_index("mp")
    d = lax.axis_index("tm")
    ntm = lax.axis_size("tm")
    swap = [(0, 1), (1, 0)]

    def partner(x):
        return lax.ppermute(x, "mp", swap)

    half = in_proj.shape[1]
    ip_o = partner(in_proj)
    r_o = partner(readout_w)
    wh_o = partner(w_hidden)
    wo_o = partner(w_out)
    emb_o = partner(action_embed)
    ip = jnp.concatenate([in_proj, ip_o], axis=1)

    rates = jnp.concatenate(
        [
            lax.dynamic_slice_in_dim(decay_rates, m * half, half),
            lax.dynamic_slice_in_dim(decay_rates, (1 - m) * half, half),
        ]
    )
    decays = jnp.exp(-rates)
    scaling = jnp.sqrt(1.0 - decays * decays)
    width = decays.shape[0]

    seqs, steps, feat = inputs.shape
    bh = seqs // 2
    x = lax.dynamic_slice_in_dim(inputs, m * bh, bh, 0)
    driven = (
        jnp.dot(x.reshape(bh * steps, feat), ip, preferred_element_type=jnp.float32).reshape(
            bh, steps, width
        )
        * scaling
    )
    my_resets = lax.dynamic_slice_in_dim(resets, m * bh, bh, 0)
    keep = (1 - my_resets).astype(jnp.float32)
    gates = keep[:, :, None] * decays
    local = local_scan(driven, gates)
    sub = steps // ntm

    positions = lax.broadcasted_iota(jnp.int32, my_resets.shape, 1)
    first = jnp.min(jnp.where(my_resets != 0, positions, steps), axis=1).astype(jnp.float32)
    ends_local = local[:, -1, :]
    ends_hi = ends_local.astype(jnp.bfloat16)
    ends_lo = (ends_local - ends_hi.astype(jnp.float32)).astype(jnp.bfloat16)
    first_rows = jnp.broadcast_to(first[:, None], (bh, width)).astype(jnp.bfloat16)
    extra = jnp.concatenate([ends_hi, ends_lo, first_rows], axis=0)
    pad_rows = -(-(extra.shape[0] + bh * sub) // 8) * 8 - bh * sub
    extra = jnp.pad(extra, ((0, pad_rows - extra.shape[0]), (0, 0)))
    states = jnp.swapaxes(local.astype(jnp.bfloat16).reshape(bh, ntm, sub, width), 0, 1)
    send = jnp.concatenate(
        [states.reshape(ntm, bh * sub, width), jnp.broadcast_to(extra[None], (ntm,) + extra.shape)],
        axis=1,
    )
    got = lax.all_to_all(send, "tm", split_axis=0, concat_axis=0, tiled=True)
    recv = jnp.swapaxes(got[:, : bh * sub].reshape(ntm, bh, sub, width), 0, 1)
    got_extra = got[:, bh * sub :]
    gathered = got_extra[:, :bh].astype(jnp.float32) + got_extra[:, bh : 2 * bh].astype(
        jnp.float32
    )
    ends = gathered
    firsts = got_extra[:, 2 * bh : 3 * bh, 0].astype(jnp.float32)

    nblocks = gathered.shape[0]
    whole_block = decays ** steps
    gain = jnp.where(firsts >= steps, 1.0, 0.0)[:, :, None] * whole_block
    total = ends
    offset = 1
    while offset < nblocks:
        gain_prev = jnp.concatenate([jnp.ones_like(gain[:offset]), gain[:-offset]], axis=0)
        total_prev = jnp.concatenate([jnp.zeros_like(total[:offset]), total[:-offset]], axis=0)
        total = gain * total_prev + total
        gain = gain * gain_prev
        offset *= 2
    carry = jnp.concatenate([jnp.zeros_like(total[:1]), total[:-1]], axis=0)

    t_glob = d * sub + lax.broadcasted_iota(jnp.int32, (sub,), 0)
    powers = decays[None, :] ** (t_glob[:, None] + 1).astype(jnp.float32)
    alive = t_glob[None, None, :].astype(jnp.float32) < jnp.swapaxes(firsts, 0, 1)[:, :, None]
    cum = jnp.where(alive[..., None], powers[None, None], 0.0)
    posterior = recv.astype(jnp.float32) + cum * jnp.swapaxes(carry, 0, 1)[:, :, None, :]

    _, blocks, _, horizon = actions.shape
    rows = bh * blocks * sub
    current = posterior.reshape(rows, width)
    my_actions = lax.dynamic_slice_in_dim(actions, m * bh, bh, 0).reshape(rows, horizon)
    table = jnp.concatenate([action_embed, emb_o], axis=1)
    table = jnp.pad(table, ((0, 128 - table.shape[0]), (0, 0)))
    one_hot = (
        jnp.swapaxes(my_actions, 0, 1)[:, :, None] == jnp.arange(128, dtype=jnp.int32)
    ).astype(jnp.bfloat16)
    vecs = jnp.stack([decays, scaling, norm_gain], axis=0)
    side = jnp.reshape(m, (1,)).astype(jnp.int32)
    keep_part, give_part = imagine(
        side, current, one_hot, vecs, readout_w, r_o, w_hidden, wh_o, table, w_out, wo_o,
        in_proj, ip_o,
    )
    got = partner(give_part)

    def arrange(part):
        return jnp.transpose(part.reshape(horizon, bh, blocks, sub, half), (1, 2, 3, 0, 4))

    mine, theirs = arrange(keep_part), arrange(got)
    first_half = jnp.where(m == 0, mine, theirs)
    second_half = jnp.where(m == 0, theirs, mine)
    return jnp.concatenate([first_half, second_half], axis=0)


def _imagine_kernel(
    side_ref, cur_ref, hot_ref, vec_ref, r_a, r_b, wh_a, wh_b, emb_ref, wo_a, wo_b, ip_a, ip_b,
    keep_ref, give_ref,
):
    horizon, rows, _ = hot_ref.shape
    half = r_a.shape[0]
    width = 2 * half
    tile = 128
    lead = side_ref[0] == 0

    def dot(a, b):
        return jnp.dot(a, b, preferred_element_type=jnp.float32)

    def chunk(c, carry):
        rs = pl.ds(pl.multiple_of(c * tile, tile), tile)
        cur_a = cur_ref[rs, :half]
        cur_b = cur_ref[rs, half:]
        for step in range(horizon):
            f = dot(cur_a.astype(jnp.bfloat16), r_a[...]).astype(jnp.bfloat16).astype(
                jnp.float32
            ) + dot(cur_b.astype(jnp.bfloat16), r_b[...]).astype(jnp.bfloat16).astype(jnp.float32)
            mean_sq = jnp.sum(f * f, axis=-1, keepdims=True) * (1.0 / width)
            normed = (f * lax.rsqrt(mean_sq + 1e-06) * vec_ref[2:3, :]).astype(jnp.bfloat16)
            hot = hot_ref[step, rs, :]
            pre_a = dot(normed, wh_a[...]) + dot(hot, emb_ref[:, :half])
            pre_b = dot(normed, wh_b[...]) + dot(hot, emb_ref[:, half:])
            hid_a = (pre_a * jax.nn.sigmoid(pre_a)).astype(jnp.bfloat16)
            hid_b = (pre_b * jax.nn.sigmoid(pre_b)).astype(jnp.bfloat16)
            lo = (dot(hid_a, wo_a[:, :half]) + dot(hid_b, wo_b[:, :half])).astype(jnp.bfloat16)
            hi = (dot(hid_a, wo_a[:, half:]) + dot(hid_b, wo_b[:, half:])).astype(jnp.bfloat16)
            keep_ref[step, rs, :] = jnp.where(lead, lo, hi)
            give_ref[step, rs, :] = jnp.where(lead, hi, lo)
            if step < horizon - 1:
                up_a = dot(lo, ip_a[:half, :]) + dot(hi, ip_a[half:, :])
                up_b = dot(lo, ip_b[:half, :]) + dot(hi, ip_b[half:, :])
                cur_a = vec_ref[0:1, :half] * cur_a + vec_ref[1:2, :half] * up_a
                cur_b = vec_ref[0:1, half:] * cur_b + vec_ref[1:2, half:] * up_b
        return carry

    lax.fori_loop(0, rows // tile, chunk, 0)


def imagine(side, current, one_hot, vecs, *weights):
    horizon, rows, _ = one_hot.shape
    half = weights[0].shape[0]
    out = jax.ShapeDtypeStruct((horizon, rows, half), jnp.bfloat16)
    vmem = pl.BlockSpec(memory_space=pltpu.VMEM)
    flops = 2 * rows * horizon * 4 * (2 * half) * (2 * half)
    return pl.pallas_call(
        _imagine_kernel,
        out_shape=(out, out),
        in_specs=[pl.BlockSpec(memory_space=pltpu.SMEM)] + [vmem] * (3 + len(weights)),
        out_specs=(vmem, vmem),
        compiler_params=pltpu.CompilerParams(vmem_limit_bytes=48 * 1024 * 1024),
        cost_estimate=pl.CostEstimate(
            flops=flops, bytes_accessed=16 * 1024 * 1024, transcendentals=rows * horizon * 2 * half
        ),
    )(side, current, one_hot, vecs, *weights)


def solution(mesh):
    in_specs = (
        P("rep", "tm", None),
        P("rep", "tm"),
        P("rep", None, "tm", None),
        P(None, "mp"),
        P(),
        P("mp", None),
        P(),
        P(None, "mp"),
        P(None, "mp"),
        P("mp", None),
    )
    out_specs = P("rep", None, "tm", None, "mp")
    return jax.shard_map(
        per_device, mesh=mesh, in_specs=in_specs, out_specs=out_specs, check_vma=False
    )
```

```python
import jax
import jax.numpy as jnp
from jax import lax
from jax.experimental import pallas as pl
from jax.experimental.pallas import tpu as pltpu
from jax.sharding import PartitionSpec as P


def _scan_kernel(x_ref, g_ref, o_ref):
    nb, steps, width = x_ref.shape

    def body(t, states):
        row = pl.ds(t, 1)
        new = []
        for b in range(nb):
            h = g_ref[b, row, :] * states[b] + x_ref[b, row, :]
            o_ref[b, row, :] = h
            new.append(h)
        return tuple(new)

    start = tuple(jnp.zeros((1, width), jnp.float32) for _ in range(nb))
    lax.fori_loop(0, steps, body, start, unroll=8)


def local_scan(driven, gates):
    size = driven.size
    return pl.pallas_call(
        _scan_kernel,
        out_shape=jax.ShapeDtypeStruct(driven.shape, jnp.float32),
        in_specs=[pl.BlockSpec(memory_space=pltpu.VMEM)] * 2,
        out_specs=pl.BlockSpec(memory_space=pltpu.VMEM),
        cost_estimate=pl.CostEstimate(flops=2 * size, bytes_accessed=12 * size, transcendentals=0),
    )(driven, gates)


def gather_blocks(value, axis, mine, count):
    if count & (count - 1):
        return lax.all_gather(value, axis)
    held = value[None]
    shift = 1
    while shift < count:
        pairs = [(i, (i + shift) % count) for i in range(count)]
        held = jnp.concatenate([held, lax.ppermute(held, axis, pairs)], axis=0)
        shift *= 2
    order = (mine - jnp.arange(count, dtype=jnp.int32)) % count
    return jnp.take(held, order, axis=0)


def per_device(
    inputs,
    resets,
    actions,
    in_proj,
    decay_rates,
    readout_w,
    norm_gain,
    w_hidden,
    action_embed,
    w_out,
):
    m = lax.axis_index("mp")
    d = lax.axis_index("tm")
    ntm = lax.axis_size("tm")
    swap = [(0, 1), (1, 0)]

    def partner(x):
        return lax.ppermute(x, "mp", swap)

    half = in_proj.shape[1]
    ip_o = partner(in_proj)
    r_o = partner(readout_w)
    wh_o = partner(w_hidden)
    wo_o = partner(w_out)
    emb_o = partner(action_embed)
    ip = jnp.concatenate([in_proj, ip_o], axis=1)

    rates = jnp.concatenate(
        [
            lax.dynamic_slice_in_dim(decay_rates, m * half, half),
            lax.dynamic_slice_in_dim(decay_rates, (1 - m) * half, half),
        ]
    )
    decays = jnp.exp(-rates)
    scaling = jnp.sqrt(1.0 - decays * decays)
    width = decays.shape[0]

    seqs, steps, feat = inputs.shape
    bh = seqs // 2
    x = lax.dynamic_slice_in_dim(inputs, m * bh, bh, 0)
    driven = (
        jnp.dot(x.reshape(bh * steps, feat), ip, preferred_element_type=jnp.float32).reshape(
            bh, steps, width
        )
        * scaling
    )
    all_resets = lax.dynamic_slice_in_dim(resets, m * bh, bh, 0)
    nblocks = all_resets.shape[1] // steps
    block_resets = all_resets.reshape(bh, nblocks, steps)
    my_resets = lax.dynamic_index_in_dim(block_resets, d, axis=1, keepdims=False)
    keep = (1 - my_resets).astype(jnp.float32)
    gates = keep[:, :, None] * decays
    local = local_scan(driven, gates)
    sub = steps // ntm

    positions = lax.broadcasted_iota(jnp.int32, block_resets.shape, 2)
    firsts = jnp.swapaxes(
        jnp.min(jnp.where(block_resets != 0, positions, steps), axis=2), 0, 1
    ).astype(jnp.float32)

    ends_local = local[:, -1, :]
    ends_hi = ends_local.astype(jnp.bfloat16)
    ends_lo = (ends_local - ends_hi.astype(jnp.float32)).astype(jnp.bfloat16)
    extra = jnp.concatenate([ends_hi, ends_lo], axis=0).reshape(-1)
    rows_sent = bh * sub
    lanes = -(-extra.shape[0] // (rows_sent * 128)) * 128
    extra = jnp.pad(extra, (0, rows_sent * lanes - extra.shape[0])).reshape(rows_sent, lanes)
    states = jnp.swapaxes(local.astype(jnp.bfloat16).reshape(bh, ntm, sub, width), 0, 1)
    send = jnp.concatenate(
        [states.reshape(ntm, rows_sent, width), jnp.broadcast_to(extra[None], (ntm,) + extra.shape)],
        axis=2,
    )
    got = lax.all_to_all(send, "tm", split_axis=0, concat_axis=0, tiled=True)
    recv = jnp.swapaxes(got[:, :, :width].reshape(ntm, bh, sub, width), 0, 1)
    got_extra = got[:, :, width:].reshape(ntm, -1)[:, : 2 * bh * width].reshape(ntm, 2, bh, width)
    gathered = got_extra[:, 0].astype(jnp.float32) + got_extra[:, 1].astype(jnp.float32)
    ends = gathered

    nblocks = gathered.shape[0]
    whole_block = decays ** steps
    gain = jnp.where(firsts >= steps, 1.0, 0.0)[:, :, None] * whole_block
    total = ends
    offset = 1
    while offset < nblocks:
        gain_prev = jnp.concatenate([jnp.ones_like(gain[:offset]), gain[:-offset]], axis=0)
        total_prev = jnp.concatenate([jnp.zeros_like(total[:offset]), total[:-offset]], axis=0)
        total = gain * total_prev + total
        gain = gain * gain_prev
        offset *= 2
    carry = jnp.concatenate([jnp.zeros_like(total[:1]), total[:-1]], axis=0)

    t_glob = d * sub + lax.broadcasted_iota(jnp.int32, (sub,), 0)
    powers = decays[None, :] ** (t_glob[:, None] + 1).astype(jnp.float32)
    alive = t_glob[None, None, :].astype(jnp.float32) < jnp.swapaxes(firsts, 0, 1)[:, :, None]
    cum = jnp.where(alive[..., None], powers[None, None], 0.0)
    posterior = recv.astype(jnp.float32) + cum * jnp.swapaxes(carry, 0, 1)[:, :, None, :]

    _, blocks, _, horizon = actions.shape
    rows = bh * blocks * sub
    current = posterior.reshape(rows, width)
    my_actions = lax.dynamic_slice_in_dim(actions, m * bh, bh, 0).reshape(rows, horizon)
    table = jnp.concatenate([action_embed, emb_o], axis=1)
    table = jnp.pad(table, ((0, 128 - table.shape[0]), (0, 0)))
    one_hot = (
        jnp.swapaxes(my_actions, 0, 1)[:, :, None] == jnp.arange(128, dtype=jnp.int32)
    ).astype(jnp.bfloat16)
    vecs = jnp.stack([decays, scaling, norm_gain], axis=0)
    side = jnp.reshape(m, (1,)).astype(jnp.int32)
    keep_part, give_part = imagine(
        side, current, one_hot, vecs, readout_w, r_o, w_hidden, wh_o, table, w_out, wo_o,
        in_proj, ip_o,
    )
    got = partner(give_part)

    def arrange(part):
        return jnp.transpose(part.reshape(horizon, bh, blocks, sub, half), (1, 2, 3, 0, 4))

    mine, theirs = arrange(keep_part), arrange(got)
    first_half = jnp.where(m == 0, mine, theirs)
    second_half = jnp.where(m == 0, theirs, mine)
    return jnp.concatenate([first_half, second_half], axis=0)


def _imagine_kernel(
    side_ref, cur_ref, hot_ref, vec_ref, r_a, r_b, wh_a, wh_b, emb_ref, wo_a, wo_b, ip_a, ip_b,
    keep_ref, give_ref,
):
    horizon, rows, _ = hot_ref.shape
    half = r_a.shape[0]
    width = 2 * half
    tile = 128
    lead = side_ref[0] == 0

    def dot(a, b):
        return jnp.dot(a, b, preferred_element_type=jnp.float32)

    def chunk(c, carry):
        rs = pl.ds(pl.multiple_of(c * tile, tile), tile)
        cur_a = cur_ref[rs, :half]
        cur_b = cur_ref[rs, half:]
        for step in range(horizon):
            f = dot(cur_a.astype(jnp.bfloat16), r_a[...]).astype(jnp.bfloat16).astype(
                jnp.float32
            ) + dot(cur_b.astype(jnp.bfloat16), r_b[...]).astype(jnp.bfloat16).astype(jnp.float32)
            mean_sq = jnp.sum(f * f, axis=-1, keepdims=True) * (1.0 / width)
            normed = (f * lax.rsqrt(mean_sq + 1e-06) * vec_ref[2:3, :]).astype(jnp.bfloat16)
            hot = hot_ref[step, rs, :]
            pre_a = dot(normed, wh_a[...]) + dot(hot, emb_ref[:, :half])
            pre_b = dot(normed, wh_b[...]) + dot(hot, emb_ref[:, half:])
            hid_a = (pre_a * jax.nn.sigmoid(pre_a)).astype(jnp.bfloat16)
            hid_b = (pre_b * jax.nn.sigmoid(pre_b)).astype(jnp.bfloat16)
            lo = (dot(hid_a, wo_a[:, :half]) + dot(hid_b, wo_b[:, :half])).astype(jnp.bfloat16)
            hi = (dot(hid_a, wo_a[:, half:]) + dot(hid_b, wo_b[:, half:])).astype(jnp.bfloat16)
            keep_ref[step, rs, :] = jnp.where(lead, lo, hi)
            give_ref[step, rs, :] = jnp.where(lead, hi, lo)
            if step < horizon - 1:
                up_a = dot(lo, ip_a[:half, :]) + dot(hi, ip_a[half:, :])
                up_b = dot(lo, ip_b[:half, :]) + dot(hi, ip_b[half:, :])
                cur_a = vec_ref[0:1, :half] * cur_a + vec_ref[1:2, :half] * up_a
                cur_b = vec_ref[0:1, half:] * cur_b + vec_ref[1:2, half:] * up_b
        return carry

    lax.fori_loop(0, rows // tile, chunk, 0)


def imagine(side, current, one_hot, vecs, *weights):
    horizon, rows, _ = one_hot.shape
    half = weights[0].shape[0]
    out = jax.ShapeDtypeStruct((horizon, rows, half), jnp.bfloat16)
    vmem = pl.BlockSpec(memory_space=pltpu.VMEM)
    flops = 2 * rows * horizon * 4 * (2 * half) * (2 * half)
    return pl.pallas_call(
        _imagine_kernel,
        out_shape=(out, out),
        in_specs=[pl.BlockSpec(memory_space=pltpu.SMEM)] + [vmem] * (3 + len(weights)),
        out_specs=(vmem, vmem),
        compiler_params=pltpu.CompilerParams(vmem_limit_bytes=48 * 1024 * 1024),
        cost_estimate=pl.CostEstimate(
            flops=flops, bytes_accessed=16 * 1024 * 1024, transcendentals=rows * horizon * 2 * half
        ),
    )(side, current, one_hot, vecs, *weights)


def solution(mesh):
    in_specs = (
        P("rep", "tm", None),
        P("rep", None),
        P("rep", None, "tm", None),
        P(None, "mp"),
        P(),
        P("mp", None),
        P(),
        P(None, "mp"),
        P(None, "mp"),
        P("mp", None),
    )
    out_specs = P("rep", None, "tm", None, "mp")
    return jax.shard_map(
        per_device, mesh=mesh, in_specs=in_specs, out_specs=out_specs, check_vma=False
    )
```

```python
import jax
import jax.numpy as jnp
from jax import lax
from jax.experimental import pallas as pl
from jax.experimental.pallas import tpu as pltpu
from jax.sharding import PartitionSpec as P


def _scan_kernel(x_ref, g_ref, o_ref):
    nb, steps, width = x_ref.shape

    def body(t, states):
        row = pl.ds(t, 1)
        new = []
        for b in range(nb):
            h = g_ref[b, row, :] * states[b] + x_ref[b, row, :]
            o_ref[b, row, :] = h
            new.append(h)
        return tuple(new)

    start = tuple(jnp.zeros((1, width), jnp.float32) for _ in range(nb))
    lax.fori_loop(0, steps, body, start, unroll=8)


def local_scan(driven, gates):
    size = driven.size
    return pl.pallas_call(
        _scan_kernel,
        out_shape=jax.ShapeDtypeStruct(driven.shape, jnp.float32),
        in_specs=[pl.BlockSpec(memory_space=pltpu.VMEM)] * 2,
        out_specs=pl.BlockSpec(memory_space=pltpu.VMEM),
        cost_estimate=pl.CostEstimate(flops=2 * size, bytes_accessed=12 * size, transcendentals=0),
    )(driven, gates)


def gather_blocks(value, axis, mine, count):
    if count & (count - 1):
        return lax.all_gather(value, axis)
    held = value[None]
    shift = 1
    while shift < count:
        pairs = [(i, (i + shift) % count) for i in range(count)]
        held = jnp.concatenate([held, lax.ppermute(held, axis, pairs)], axis=0)
        shift *= 2
    order = (mine - jnp.arange(count, dtype=jnp.int32)) % count
    return jnp.take(held, order, axis=0)


def per_device(
    inputs,
    resets,
    actions,
    in_proj,
    decay_rates,
    readout_w,
    norm_gain,
    w_hidden,
    action_embed,
    w_out,
):
    m = lax.axis_index("mp")
    d = lax.axis_index("tm")
    ntm = lax.axis_size("tm")
    swap = [(0, 1), (1, 0)]

    def partner(x):
        return lax.ppermute(x, "mp", swap)

    half = in_proj.shape[1]
    ip_o = partner(in_proj)
    r_o = partner(readout_w)
    wh_o = partner(w_hidden)
    wo_o = partner(w_out)
    emb_o = partner(action_embed)
    ip = jnp.concatenate([in_proj, ip_o], axis=1)

    rates = jnp.concatenate(
        [
            lax.dynamic_slice_in_dim(decay_rates, m * half, half),
            lax.dynamic_slice_in_dim(decay_rates, (1 - m) * half, half),
        ]
    )
    decays = jnp.exp(-rates)
    scaling = jnp.sqrt(1.0 - decays * decays)
    width = decays.shape[0]

    seqs, steps, feat = inputs.shape
    bh = seqs // 2
    x = lax.dynamic_slice_in_dim(inputs, m * bh, bh, 0)
    driven = (
        jnp.dot(x.reshape(bh * steps, feat), ip, preferred_element_type=jnp.float32).reshape(
            bh, steps, width
        )
        * scaling
    )
    my_resets = lax.dynamic_slice_in_dim(resets, m * bh, bh, 0)
    keep = (1 - my_resets).astype(jnp.float32)
    gates = keep[:, :, None] * decays
    local = local_scan(driven, gates)
    sub = steps // ntm
    positions = lax.broadcasted_iota(jnp.int32, my_resets.shape, 1)
    first = jnp.min(jnp.where(my_resets != 0, positions, steps), axis=1).astype(jnp.float32)

    ends_local = local[:, -1, :]
    ends_hi = ends_local.astype(jnp.bfloat16)
    ends_lo = (ends_local - ends_hi.astype(jnp.float32)).astype(jnp.bfloat16)
    rows_sent = bh * sub
    lanes = -(-(2 * bh * width) // (rows_sent * 128)) * 128
    room = rows_sent * lanes - bh * width - bh
    lo_flat = ends_lo.reshape(-1)[:room]
    extra = jnp.concatenate(
        [ends_hi.reshape(-1), first.astype(jnp.bfloat16), lo_flat]
    )
    extra = jnp.pad(extra, (0, rows_sent * lanes - extra.shape[0])).reshape(rows_sent, lanes)
    states = jnp.swapaxes(local.astype(jnp.bfloat16).reshape(bh, ntm, sub, width), 0, 1)
    send = jnp.concatenate(
        [states.reshape(ntm, rows_sent, width), jnp.broadcast_to(extra[None], (ntm,) + extra.shape)],
        axis=2,
    )
    got = lax.all_to_all(send, "tm", split_axis=0, concat_axis=0, tiled=True)
    recv = jnp.swapaxes(got[:, :, :width].reshape(ntm, bh, sub, width), 0, 1)
    flat = got[:, :, width:].reshape(ntm, -1)
    got_hi = flat[:, : bh * width].astype(jnp.float32)
    firsts = flat[:, bh * width : bh * width + bh].astype(jnp.float32)
    got_lo = flat[:, bh * width + bh : bh * width + bh + lo_flat.shape[0]].astype(jnp.float32)
    got_lo = jnp.pad(got_lo, ((0, 0), (0, bh * width - lo_flat.shape[0])))
    gathered = (got_hi + got_lo).reshape(ntm, bh, width)
    ends = gathered

    nblocks = gathered.shape[0]
    whole_block = decays ** steps
    gain = jnp.where(firsts >= steps, 1.0, 0.0)[:, :, None] * whole_block
    total = ends
    offset = 1
    while offset < nblocks:
        gain_prev = jnp.concatenate([jnp.ones_like(gain[:offset]), gain[:-offset]], axis=0)
        total_prev = jnp.concatenate([jnp.zeros_like(total[:offset]), total[:-offset]], axis=0)
        total = gain * total_prev + total
        gain = gain * gain_prev
        offset *= 2
    carry = jnp.concatenate([jnp.zeros_like(total[:1]), total[:-1]], axis=0)

    t_glob = d * sub + lax.broadcasted_iota(jnp.int32, (sub,), 0)
    powers = decays[None, :] ** (t_glob[:, None] + 1).astype(jnp.float32)
    alive = t_glob[None, None, :].astype(jnp.float32) < jnp.swapaxes(firsts, 0, 1)[:, :, None]
    cum = jnp.where(alive[..., None], powers[None, None], 0.0)
    posterior = recv.astype(jnp.float32) + cum * jnp.swapaxes(carry, 0, 1)[:, :, None, :]

    _, blocks, _, horizon = actions.shape
    rows = bh * blocks * sub
    current = posterior.reshape(rows, width)
    my_actions = lax.dynamic_slice_in_dim(actions, m * bh, bh, 0).reshape(rows, horizon)
    table = jnp.concatenate([action_embed, emb_o], axis=1)
    table = jnp.pad(table, ((0, 128 - table.shape[0]), (0, 0)))
    one_hot = (
        jnp.swapaxes(my_actions, 0, 1)[:, :, None] == jnp.arange(128, dtype=jnp.int32)
    ).astype(jnp.bfloat16)
    vecs = jnp.stack([decays, scaling, norm_gain], axis=0)
    side = jnp.reshape(m, (1,)).astype(jnp.int32)
    keep_part, give_part = imagine(
        side, current, one_hot, vecs, readout_w, r_o, w_hidden, wh_o, table, w_out, wo_o,
        in_proj, ip_o,
    )
    got = partner(give_part)

    def arrange(part):
        return jnp.transpose(part.reshape(horizon, bh, blocks, sub, half), (1, 2, 3, 0, 4))

    mine, theirs = arrange(keep_part), arrange(got)
    first_half = jnp.where(m == 0, mine, theirs)
    second_half = jnp.where(m == 0, theirs, mine)
    return jnp.concatenate([first_half, second_half], axis=0)


def _imagine_kernel(
    side_ref, cur_ref, hot_ref, vec_ref, r_a, r_b, wh_a, wh_b, emb_ref, wo_a, wo_b, ip_a, ip_b,
    keep_ref, give_ref,
):
    horizon, rows, _ = hot_ref.shape
    half = r_a.shape[0]
    width = 2 * half
    tile = 128
    lead = side_ref[0] == 0

    def dot(a, b):
        return jnp.dot(a, b, preferred_element_type=jnp.float32)

    def chunk(c, carry):
        rs = pl.ds(pl.multiple_of(c * tile, tile), tile)
        cur_a = cur_ref[rs, :half]
        cur_b = cur_ref[rs, half:]
        for step in range(horizon):
            f = dot(cur_a.astype(jnp.bfloat16), r_a[...]).astype(jnp.bfloat16).astype(
                jnp.float32
            ) + dot(cur_b.astype(jnp.bfloat16), r_b[...]).astype(jnp.bfloat16).astype(jnp.float32)
            mean_sq = jnp.sum(f * f, axis=-1, keepdims=True) * (1.0 / width)
            normed = (f * lax.rsqrt(mean_sq + 1e-06) * vec_ref[2:3, :]).astype(jnp.bfloat16)
            hot = hot_ref[step, rs, :]
            pre_a = dot(normed, wh_a[...]) + dot(hot, emb_ref[:, :half])
            pre_b = dot(normed, wh_b[...]) + dot(hot, emb_ref[:, half:])
            hid_a = (pre_a * jax.nn.sigmoid(pre_a)).astype(jnp.bfloat16)
            hid_b = (pre_b * jax.nn.sigmoid(pre_b)).astype(jnp.bfloat16)
            lo = (dot(hid_a, wo_a[:, :half]) + dot(hid_b, wo_b[:, :half])).astype(jnp.bfloat16)
            hi = (dot(hid_a, wo_a[:, half:]) + dot(hid_b, wo_b[:, half:])).astype(jnp.bfloat16)
            keep_ref[step, rs, :] = jnp.where(lead, lo, hi)
            give_ref[step, rs, :] = jnp.where(lead, hi, lo)
            if step < horizon - 1:
                up_a = dot(lo, ip_a[:half, :]) + dot(hi, ip_a[half:, :])
                up_b = dot(lo, ip_b[:half, :]) + dot(hi, ip_b[half:, :])
                cur_a = vec_ref[0:1, :half] * cur_a + vec_ref[1:2, :half] * up_a
                cur_b = vec_ref[0:1, half:] * cur_b + vec_ref[1:2, half:] * up_b
        return carry

    lax.fori_loop(0, rows // tile, chunk, 0)


def imagine(side, current, one_hot, vecs, *weights):
    horizon, rows, _ = one_hot.shape
    half = weights[0].shape[0]
    out = jax.ShapeDtypeStruct((horizon, rows, half), jnp.bfloat16)
    vmem = pl.BlockSpec(memory_space=pltpu.VMEM)
    flops = 2 * rows * horizon * 4 * (2 * half) * (2 * half)
    return pl.pallas_call(
        _imagine_kernel,
        out_shape=(out, out),
        in_specs=[pl.BlockSpec(memory_space=pltpu.SMEM)] + [vmem] * (3 + len(weights)),
        out_specs=(vmem, vmem),
        compiler_params=pltpu.CompilerParams(vmem_limit_bytes=48 * 1024 * 1024),
        cost_estimate=pl.CostEstimate(
            flops=flops, bytes_accessed=16 * 1024 * 1024, transcendentals=rows * horizon * 2 * half
        ),
    )(side, current, one_hot, vecs, *weights)


def solution(mesh):
    in_specs = (
        P("rep", "tm", None),
        P("rep", "tm"),
        P("rep", None, "tm", None),
        P(None, "mp"),
        P(),
        P("mp", None),
        P(),
        P(None, "mp"),
        P(None, "mp"),
        P("mp", None),
    )
    out_specs = P("rep", None, "tm", None, "mp")
    return jax.shard_map(
        per_device, mesh=mesh, in_specs=in_specs, out_specs=out_specs, check_vma=False
    )
```

```python
import jax
import jax.numpy as jnp
from jax import lax
from jax.experimental import pallas as pl
from jax.experimental.pallas import tpu as pltpu
from jax.sharding import PartitionSpec as P


def _scan_kernel(x_ref, g_ref, o_ref):
    nb, steps, width = x_ref.shape

    def body(t, states):
        row = pl.ds(t, 1)
        new = []
        for b in range(nb):
            h = g_ref[b, row, :] * states[b] + x_ref[b, row, :]
            o_ref[b, row, :] = h
            new.append(h)
        return tuple(new)

    start = tuple(jnp.zeros((1, width), jnp.float32) for _ in range(nb))
    lax.fori_loop(0, steps, body, start, unroll=8)


def local_scan(driven, gates):
    size = driven.size
    return pl.pallas_call(
        _scan_kernel,
        out_shape=jax.ShapeDtypeStruct(driven.shape, jnp.float32),
        in_specs=[pl.BlockSpec(memory_space=pltpu.VMEM)] * 2,
        out_specs=pl.BlockSpec(memory_space=pltpu.VMEM),
        cost_estimate=pl.CostEstimate(flops=2 * size, bytes_accessed=12 * size, transcendentals=0),
    )(driven, gates)


def gather_blocks(value, axis, mine, count):
    if count & (count - 1):
        return lax.all_gather(value, axis)
    held = value[None]
    shift = 1
    while shift < count:
        pairs = [(i, (i + shift) % count) for i in range(count)]
        held = jnp.concatenate([held, lax.ppermute(held, axis, pairs)], axis=0)
        shift *= 2
    order = (mine - jnp.arange(count, dtype=jnp.int32)) % count
    return jnp.take(held, order, axis=0)


def per_device(
    inputs,
    resets,
    actions,
    in_proj,
    decay_rates,
    readout_w,
    norm_gain,
    w_hidden,
    action_embed,
    w_out,
):
    m = lax.axis_index("mp")
    d = lax.axis_index("tm")
    ntm = lax.axis_size("tm")
    swap = [(0, 1), (1, 0)]

    def partner(x):
        return lax.ppermute(x, "mp", swap)

    half = in_proj.shape[1]
    ip_o = partner(in_proj)
    r_o = partner(readout_w)
    wh_o = partner(w_hidden)
    wo_o = partner(w_out)
    emb_o = partner(action_embed)
    ip = jnp.concatenate([in_proj, ip_o], axis=1)

    rates = jnp.concatenate(
        [
            lax.dynamic_slice_in_dim(decay_rates, m * half, half),
            lax.dynamic_slice_in_dim(decay_rates, (1 - m) * half, half),
        ]
    )
    decays = jnp.exp(-rates)
    scaling = jnp.sqrt(1.0 - decays * decays)
    width = decays.shape[0]

    seqs, steps, feat = inputs.shape
    bh = seqs // 2
    x = lax.dynamic_slice_in_dim(inputs, m * bh, bh, 0)
    driven = (
        jnp.dot(x.reshape(bh * steps, feat), ip, preferred_element_type=jnp.float32).reshape(
            bh, steps, width
        )
        * scaling
    )
    my_resets = lax.dynamic_slice_in_dim(resets, m * bh, bh, 0)
    keep = (1 - my_resets).astype(jnp.float32)
    gates = keep[:, :, None] * decays
    local = local_scan(driven, gates)
    sub = steps // ntm
    positions = lax.broadcasted_iota(jnp.int32, my_resets.shape, 1)
    first = jnp.min(jnp.where(my_resets != 0, positions, steps), axis=1).astype(jnp.float32)

    ends_local = local[:, -1, :]
    ends_hi = ends_local.astype(jnp.bfloat16)
    ends_lo = (ends_local - ends_hi.astype(jnp.float32)).astype(jnp.bfloat16)
    rows_sent = bh * sub
    lanes = -(-(2 * bh * width) // (rows_sent * 128)) * 128
    room = rows_sent * lanes - bh * width - bh
    lo_flat = ends_lo.reshape(-1)[:room]
    extra = jnp.concatenate(
        [ends_hi.reshape(-1), first.astype(jnp.bfloat16), lo_flat]
    )
    extra = jnp.pad(extra, (0, rows_sent * lanes - extra.shape[0])).reshape(rows_sent, lanes)
    states = jnp.swapaxes(local.astype(jnp.bfloat16).reshape(bh, ntm, sub, width), 0, 1)
    send = jnp.concatenate(
        [states.reshape(ntm, rows_sent, width), jnp.broadcast_to(extra[None], (ntm,) + extra.shape)],
        axis=2,
    )
    got = lax.all_to_all(send, "tm", split_axis=0, concat_axis=0, tiled=True)
    recv = jnp.swapaxes(got[:, :, :width].reshape(ntm, bh, sub, width), 0, 1)
    flat = got[:, :, width:].reshape(ntm, -1)
    got_hi = flat[:, : bh * width].astype(jnp.float32)
    firsts = flat[:, bh * width : bh * width + bh].astype(jnp.float32)
    got_lo = flat[:, bh * width + bh : bh * width + bh + lo_flat.shape[0]].astype(jnp.float32)
    got_lo = jnp.pad(got_lo, ((0, 0), (0, bh * width - lo_flat.shape[0])))
    gathered = (got_hi + got_lo).reshape(ntm, bh, width)
    ends = gathered

    nblocks = gathered.shape[0]
    whole_block = decays ** steps
    gain = jnp.where(firsts >= steps, 1.0, 0.0)[:, :, None] * whole_block
    total = ends
    offset = 1
    while offset < nblocks:
        gain_prev = jnp.concatenate([jnp.ones_like(gain[:offset]), gain[:-offset]], axis=0)
        total_prev = jnp.concatenate([jnp.zeros_like(total[:offset]), total[:-offset]], axis=0)
        total = gain * total_prev + total
        gain = gain * gain_prev
        offset *= 2
    carry = jnp.concatenate([jnp.zeros_like(total[:1]), total[:-1]], axis=0)

    t_glob = d * sub + lax.broadcasted_iota(jnp.int32, (sub,), 0)
    powers = decays[None, :] ** (t_glob[:, None] + 1).astype(jnp.float32)
    alive = t_glob[None, None, :].astype(jnp.float32) < jnp.swapaxes(firsts, 0, 1)[:, :, None]
    cum = jnp.where(alive[..., None], powers[None, None], 0.0)
    posterior = recv.astype(jnp.float32) + cum * jnp.swapaxes(carry, 0, 1)[:, :, None, :]

    _, blocks, _, horizon = actions.shape
    rows = bh * blocks * sub
    current = posterior.reshape(rows, width)
    my_actions = lax.dynamic_slice_in_dim(actions, m * bh, bh, 0).reshape(rows, horizon)
    table = jnp.concatenate([action_embed, emb_o], axis=1)
    table = jnp.pad(table, ((0, 128 - table.shape[0]), (0, 0)))
    one_hot = (
        jnp.swapaxes(my_actions, 0, 1)[:, :, None] == jnp.arange(128, dtype=jnp.int32)
    ).astype(jnp.bfloat16)
    vecs = jnp.stack([decays, scaling, norm_gain], axis=0)
    side = jnp.reshape(m, (1,)).astype(jnp.int32)
    keep_part, give_part = imagine(
        side, current, one_hot, vecs, readout_w, r_o, w_hidden, wh_o, table, w_out, wo_o,
        in_proj, ip_o,
    )
    got = partner(give_part)

    def arrange(part):
        return part.reshape(bh, blocks, sub, horizon, half)

    mine, theirs = arrange(keep_part), arrange(got)
    first_half = jnp.where(m == 0, mine, theirs)
    second_half = jnp.where(m == 0, theirs, mine)
    return jnp.concatenate([first_half, second_half], axis=0)


def _imagine_kernel(
    side_ref, cur_ref, hot_ref, vec_ref, r_a, r_b, wh_a, wh_b, emb_ref, wo_a, wo_b, ip_a, ip_b,
    keep_ref, give_ref,
):
    horizon, rows, _ = hot_ref.shape
    half = r_a.shape[0]
    width = 2 * half
    tile = 128
    lead = side_ref[0] == 0

    def dot(a, b):
        return jnp.dot(a, b, preferred_element_type=jnp.float32)

    def chunk(c, carry):
        rs = pl.ds(pl.multiple_of(c * tile, tile), tile)
        cur_a = cur_ref[rs, :half]
        cur_b = cur_ref[rs, half:]
        for step in range(horizon):
            f = dot(cur_a.astype(jnp.bfloat16), r_a[...]).astype(jnp.bfloat16).astype(
                jnp.float32
            ) + dot(cur_b.astype(jnp.bfloat16), r_b[...]).astype(jnp.bfloat16).astype(jnp.float32)
            mean_sq = jnp.sum(f * f, axis=-1, keepdims=True) * (1.0 / width)
            normed = (f * lax.rsqrt(mean_sq + 1e-06) * vec_ref[2:3, :]).astype(jnp.bfloat16)
            hot = hot_ref[step, rs, :]
            pre_a = dot(normed, wh_a[...]) + dot(hot, emb_ref[:, :half])
            pre_b = dot(normed, wh_b[...]) + dot(hot, emb_ref[:, half:])
            hid_a = (pre_a * jax.nn.sigmoid(pre_a)).astype(jnp.bfloat16)
            hid_b = (pre_b * jax.nn.sigmoid(pre_b)).astype(jnp.bfloat16)
            lo = (dot(hid_a, wo_a[:, :half]) + dot(hid_b, wo_b[:, :half])).astype(jnp.bfloat16)
            hi = (dot(hid_a, wo_a[:, half:]) + dot(hid_b, wo_b[:, half:])).astype(jnp.bfloat16)
            cols = pl.ds(step * half, half)
            keep_ref[rs, cols] = jnp.where(lead, lo, hi)
            give_ref[rs, cols] = jnp.where(lead, hi, lo)
            if step < horizon - 1:
                up_a = dot(lo, ip_a[:half, :]) + dot(hi, ip_a[half:, :])
                up_b = dot(lo, ip_b[:half, :]) + dot(hi, ip_b[half:, :])
                cur_a = vec_ref[0:1, :half] * cur_a + vec_ref[1:2, :half] * up_a
                cur_b = vec_ref[0:1, half:] * cur_b + vec_ref[1:2, half:] * up_b
        return carry

    lax.fori_loop(0, rows // tile, chunk, 0)


def imagine(side, current, one_hot, vecs, *weights):
    horizon, rows, _ = one_hot.shape
    half = weights[0].shape[0]
    out = jax.ShapeDtypeStruct((rows, horizon * half), jnp.bfloat16)
    vmem = pl.BlockSpec(memory_space=pltpu.VMEM)
    flops = 2 * rows * horizon * 4 * (2 * half) * (2 * half)
    return pl.pallas_call(
        _imagine_kernel,
        out_shape=(out, out),
        in_specs=[pl.BlockSpec(memory_space=pltpu.SMEM)] + [vmem] * (3 + len(weights)),
        out_specs=(vmem, vmem),
        compiler_params=pltpu.CompilerParams(vmem_limit_bytes=48 * 1024 * 1024),
        cost_estimate=pl.CostEstimate(
            flops=flops, bytes_accessed=16 * 1024 * 1024, transcendentals=rows * horizon * 2 * half
        ),
    )(side, current, one_hot, vecs, *weights)


def solution(mesh):
    in_specs = (
        P("rep", "tm", None),
        P("rep", "tm"),
        P("rep", None, "tm", None),
        P(None, "mp"),
        P(),
        P("mp", None),
        P(),
        P(None, "mp"),
        P(None, "mp"),
        P("mp", None),
    )
    out_specs = P("rep", None, "tm", None, "mp")
    return jax.shard_map(
        per_device, mesh=mesh, in_specs=in_specs, out_specs=out_specs, check_vma=False
    )
```

```python
import jax
import jax.numpy as jnp
from jax import lax
from jax.experimental import pallas as pl
from jax.experimental.pallas import tpu as pltpu
from jax.sharding import PartitionSpec as P


def _scan_kernel(x_ref, g_ref, o_ref):
    nb, steps, width = x_ref.shape

    def body(t, states):
        row = pl.ds(t, 1)
        new = []
        for b in range(nb):
            h = g_ref[b, row, :] * states[b] + x_ref[b, row, :]
            o_ref[b, row, :] = h
            new.append(h)
        return tuple(new)

    start = tuple(jnp.zeros((1, width), jnp.float32) for _ in range(nb))
    lax.fori_loop(0, steps, body, start, unroll=8)


def local_scan(driven, gates):
    size = driven.size
    return pl.pallas_call(
        _scan_kernel,
        out_shape=jax.ShapeDtypeStruct(driven.shape, jnp.float32),
        in_specs=[pl.BlockSpec(memory_space=pltpu.VMEM)] * 2,
        out_specs=pl.BlockSpec(memory_space=pltpu.VMEM),
        cost_estimate=pl.CostEstimate(flops=2 * size, bytes_accessed=12 * size, transcendentals=0),
    )(driven, gates)


def gather_blocks(value, axis, mine, count):
    if count & (count - 1):
        return lax.all_gather(value, axis)
    held = value[None]
    shift = 1
    while shift < count:
        pairs = [(i, (i + shift) % count) for i in range(count)]
        held = jnp.concatenate([held, lax.ppermute(held, axis, pairs)], axis=0)
        shift *= 2
    order = (mine - jnp.arange(count, dtype=jnp.int32)) % count
    return jnp.take(held, order, axis=0)


def per_device(
    inputs,
    resets,
    actions,
    in_proj,
    decay_rates,
    readout_w,
    norm_gain,
    w_hidden,
    action_embed,
    w_out,
):
    m = lax.axis_index("mp")
    d = lax.axis_index("tm")
    ntm = lax.axis_size("tm")
    swap = [(0, 1), (1, 0)]

    def partner(x):
        return lax.ppermute(x, "mp", swap)

    half = in_proj.shape[1]
    ip_o = partner(in_proj)
    r_o = partner(readout_w)
    wh_o = partner(w_hidden)
    wo_o = partner(w_out)
    emb_o = partner(action_embed)
    ip = jnp.concatenate([in_proj, ip_o], axis=1)

    rates = jnp.concatenate(
        [
            lax.dynamic_slice_in_dim(decay_rates, m * half, half),
            lax.dynamic_slice_in_dim(decay_rates, (1 - m) * half, half),
        ]
    )
    decays = jnp.exp(-rates)
    scaling = jnp.sqrt(1.0 - decays * decays)
    width = decays.shape[0]

    seqs, steps, feat = inputs.shape
    bh = seqs // 2
    x = lax.dynamic_slice_in_dim(inputs, m * bh, bh, 0)
    driven = (
        jnp.dot(x.reshape(bh * steps, feat), ip, preferred_element_type=jnp.float32).reshape(
            bh, steps, width
        )
        * scaling
    )
    my_resets = lax.dynamic_slice_in_dim(resets, m * bh, bh, 0)
    keep = (1 - my_resets).astype(jnp.float32)
    gates = keep[:, :, None] * decays
    local = local_scan(driven, gates)
    sub = steps // ntm
    positions = lax.broadcasted_iota(jnp.int32, my_resets.shape, 1)
    first = jnp.min(jnp.where(my_resets != 0, positions, steps), axis=1).astype(jnp.float32)

    ends_local = local[:, -1, :]
    ends_hi = ends_local.astype(jnp.bfloat16)
    ends_lo = (ends_local - ends_hi.astype(jnp.float32)).astype(jnp.bfloat16)
    rows_sent = bh * sub
    lanes = -(-(2 * bh * width) // (rows_sent * 128)) * 128
    room = rows_sent * lanes - bh * width - bh
    lo_flat = ends_lo.reshape(-1)[:room]
    extra = jnp.concatenate(
        [ends_hi.reshape(-1), first.astype(jnp.bfloat16), lo_flat]
    )
    extra = jnp.pad(extra, (0, rows_sent * lanes - extra.shape[0])).reshape(rows_sent, lanes)
    states = jnp.swapaxes(local.astype(jnp.bfloat16).reshape(bh, ntm, sub, width), 0, 1)
    send = jnp.concatenate(
        [states.reshape(ntm, rows_sent, width), jnp.broadcast_to(extra[None], (ntm,) + extra.shape)],
        axis=2,
    )
    got = lax.all_to_all(send, "tm", split_axis=0, concat_axis=0, tiled=True)
    recv = jnp.swapaxes(got[:, :, :width].reshape(ntm, bh, sub, width), 0, 1)
    flat = got[:, :, width:].reshape(ntm, -1)
    got_hi = flat[:, : bh * width].astype(jnp.float32)
    firsts = flat[:, bh * width : bh * width + bh].astype(jnp.float32)
    got_lo = flat[:, bh * width + bh : bh * width + bh + lo_flat.shape[0]].astype(jnp.float32)
    got_lo = jnp.pad(got_lo, ((0, 0), (0, bh * width - lo_flat.shape[0])))
    gathered = (got_hi + got_lo).reshape(ntm, bh, width)
    ends = gathered

    nblocks = gathered.shape[0]
    whole_block = decays ** steps
    gain = jnp.where(firsts >= steps, 1.0, 0.0)[:, :, None] * whole_block
    total = ends
    offset = 1
    while offset < nblocks:
        gain_prev = jnp.concatenate([jnp.ones_like(gain[:offset]), gain[:-offset]], axis=0)
        total_prev = jnp.concatenate([jnp.zeros_like(total[:offset]), total[:-offset]], axis=0)
        total = gain * total_prev + total
        gain = gain * gain_prev
        offset *= 2
    carry = jnp.concatenate([jnp.zeros_like(total[:1]), total[:-1]], axis=0)

    t_glob = d * sub + lax.broadcasted_iota(jnp.int32, (sub,), 0)
    powers = decays[None, :] ** (t_glob[:, None] + 1).astype(jnp.float32)
    alive = t_glob[None, None, :].astype(jnp.float32) < jnp.swapaxes(firsts, 0, 1)[:, :, None]
    cum = jnp.where(alive[..., None], powers[None, None], 0.0)
    posterior = recv.astype(jnp.float32) + cum * jnp.swapaxes(carry, 0, 1)[:, :, None, :]

    _, blocks, _, horizon = actions.shape
    rows = bh * blocks * sub
    current = posterior.reshape(rows, width)
    my_actions = lax.dynamic_slice_in_dim(actions, m * bh, bh, 0).reshape(rows, horizon)
    table = jnp.concatenate([action_embed, emb_o], axis=1)
    table = jnp.pad(table, ((0, 128 - table.shape[0]), (0, 0)))
    one_hot = (
        jnp.swapaxes(my_actions, 0, 1)[:, :, None] == jnp.arange(128, dtype=jnp.int32)
    ).astype(jnp.bfloat16)
    vecs = jnp.stack([decays, scaling, norm_gain], axis=0)
    side = jnp.reshape(m, (1,)).astype(jnp.int32)
    keep_part, give_part = imagine(
        side, current, one_hot, vecs, readout_w, r_o, w_hidden, wh_o, table, w_out, wo_o,
        in_proj, ip_o,
    )
    got = partner(give_part)

    def arrange(part):
        return jnp.transpose(part.reshape(horizon, bh, blocks, sub, half), (1, 2, 3, 0, 4))

    mine, theirs = arrange(keep_part), arrange(got)
    first_half = jnp.where(m == 0, mine, theirs)
    second_half = jnp.where(m == 0, theirs, mine)
    return jnp.concatenate([first_half, second_half], axis=0)


def _imagine_kernel(
    side_ref, cur_ref, hot_ref, vec_ref, r_a, r_b, wh_a, wh_b, emb_ref, wo_a, wo_b, ip_a, ip_b,
    keep_ref, give_ref,
):
    horizon, rows, _ = hot_ref.shape
    half = r_a.shape[0]
    width = 2 * half
    tile = 256
    lead = side_ref[0] == 0

    def dot(a, b):
        return jnp.dot(a, b, preferred_element_type=jnp.float32)

    def chunk(c, carry):
        rs = pl.ds(pl.multiple_of(c * tile, tile), tile)
        cur_a = cur_ref[rs, :half]
        cur_b = cur_ref[rs, half:]
        for step in range(horizon):
            f = dot(cur_a.astype(jnp.bfloat16), r_a[...]).astype(jnp.bfloat16).astype(
                jnp.float32
            ) + dot(cur_b.astype(jnp.bfloat16), r_b[...]).astype(jnp.bfloat16).astype(jnp.float32)
            mean_sq = jnp.sum(f * f, axis=-1, keepdims=True) * (1.0 / width)
            normed = (f * lax.rsqrt(mean_sq + 1e-06) * vec_ref[2:3, :]).astype(jnp.bfloat16)
            hot = hot_ref[step, rs, :]
            pre_a = dot(normed, wh_a[...]) + dot(hot, emb_ref[:, :half])
            pre_b = dot(normed, wh_b[...]) + dot(hot, emb_ref[:, half:])
            hid_a = (pre_a * jax.nn.sigmoid(pre_a)).astype(jnp.bfloat16)
            hid_b = (pre_b * jax.nn.sigmoid(pre_b)).astype(jnp.bfloat16)
            lo = (dot(hid_a, wo_a[:, :half]) + dot(hid_b, wo_b[:, :half])).astype(jnp.bfloat16)
            hi = (dot(hid_a, wo_a[:, half:]) + dot(hid_b, wo_b[:, half:])).astype(jnp.bfloat16)
            keep_ref[step, rs, :] = jnp.where(lead, lo, hi)
            give_ref[step, rs, :] = jnp.where(lead, hi, lo)
            if step < horizon - 1:
                up_a = dot(lo, ip_a[:half, :]) + dot(hi, ip_a[half:, :])
                up_b = dot(lo, ip_b[:half, :]) + dot(hi, ip_b[half:, :])
                cur_a = vec_ref[0:1, :half] * cur_a + vec_ref[1:2, :half] * up_a
                cur_b = vec_ref[0:1, half:] * cur_b + vec_ref[1:2, half:] * up_b
        return carry

    lax.fori_loop(0, rows // tile, chunk, 0)


def imagine(side, current, one_hot, vecs, *weights):
    horizon, rows, _ = one_hot.shape
    half = weights[0].shape[0]
    out = jax.ShapeDtypeStruct((horizon, rows, half), jnp.bfloat16)
    vmem = pl.BlockSpec(memory_space=pltpu.VMEM)
    flops = 2 * rows * horizon * 4 * (2 * half) * (2 * half)
    return pl.pallas_call(
        _imagine_kernel,
        out_shape=(out, out),
        in_specs=[pl.BlockSpec(memory_space=pltpu.SMEM)] + [vmem] * (3 + len(weights)),
        out_specs=(vmem, vmem),
        compiler_params=pltpu.CompilerParams(vmem_limit_bytes=48 * 1024 * 1024),
        cost_estimate=pl.CostEstimate(
            flops=flops, bytes_accessed=16 * 1024 * 1024, transcendentals=rows * horizon * 2 * half
        ),
    )(side, current, one_hot, vecs, *weights)


def solution(mesh):
    in_specs = (
        P("rep", "tm", None),
        P("rep", "tm"),
        P("rep", None, "tm", None),
        P(None, "mp"),
        P(),
        P("mp", None),
        P(),
        P(None, "mp"),
        P(None, "mp"),
        P("mp", None),
    )
    out_specs = P("rep", None, "tm", None, "mp")
    return jax.shard_map(
        per_device, mesh=mesh, in_specs=in_specs, out_specs=out_specs, check_vma=False
    )
```

```python
import jax
import jax.numpy as jnp
from jax import lax
from jax.experimental import pallas as pl
from jax.experimental.pallas import tpu as pltpu
from jax.sharding import PartitionSpec as P


def _scan_kernel(x_ref, g_ref, o_ref):
    nb, steps, width = x_ref.shape

    def body(t, states):
        row = pl.ds(t, 1)
        new = []
        for b in range(nb):
            h = g_ref[b, row, :] * states[b] + x_ref[b, row, :]
            o_ref[b, row, :] = h
            new.append(h)
        return tuple(new)

    start = tuple(jnp.zeros((1, width), jnp.float32) for _ in range(nb))
    lax.fori_loop(0, steps, body, start, unroll=8)


def local_scan(driven, gates):
    size = driven.size
    return pl.pallas_call(
        _scan_kernel,
        out_shape=jax.ShapeDtypeStruct(driven.shape, jnp.float32),
        in_specs=[pl.BlockSpec(memory_space=pltpu.VMEM)] * 2,
        out_specs=pl.BlockSpec(memory_space=pltpu.VMEM),
        cost_estimate=pl.CostEstimate(flops=2 * size, bytes_accessed=12 * size, transcendentals=0),
    )(driven, gates)


def gather_blocks(value, axis, mine, count):
    if count & (count - 1):
        return lax.all_gather(value, axis)
    held = value[None]
    shift = 1
    while shift < count:
        pairs = [(i, (i + shift) % count) for i in range(count)]
        held = jnp.concatenate([held, lax.ppermute(held, axis, pairs)], axis=0)
        shift *= 2
    order = (mine - jnp.arange(count, dtype=jnp.int32)) % count
    return jnp.take(held, order, axis=0)


def per_device(
    inputs,
    resets,
    actions,
    in_proj,
    decay_rates,
    readout_w,
    norm_gain,
    w_hidden,
    action_embed,
    w_out,
):
    m = lax.axis_index("mp")
    d = lax.axis_index("tm")
    ntm = lax.axis_size("tm")
    swap = [(0, 1), (1, 0)]

    def partner(x):
        return lax.ppermute(x, "mp", swap)

    half = in_proj.shape[1]
    ip_o, r_o, wh_o, wo_o, emb_o = lax.optimization_barrier(
        partner((in_proj, readout_w, w_hidden, w_out, action_embed))
    )
    ip = jnp.concatenate([in_proj, ip_o], axis=1)

    rates = jnp.concatenate(
        [
            lax.dynamic_slice_in_dim(decay_rates, m * half, half),
            lax.dynamic_slice_in_dim(decay_rates, (1 - m) * half, half),
        ]
    )
    decays = jnp.exp(-rates)
    scaling = jnp.sqrt(1.0 - decays * decays)
    width = decays.shape[0]

    seqs, steps, feat = inputs.shape
    bh = seqs // 2
    x = lax.dynamic_slice_in_dim(inputs, m * bh, bh, 0)
    driven = (
        jnp.dot(x.reshape(bh * steps, feat), ip, preferred_element_type=jnp.float32).reshape(
            bh, steps, width
        )
        * scaling
    )
    my_resets = lax.dynamic_slice_in_dim(resets, m * bh, bh, 0)
    keep = (1 - my_resets).astype(jnp.float32)
    gates = keep[:, :, None] * decays
    local = local_scan(driven, gates)
    sub = steps // ntm
    positions = lax.broadcasted_iota(jnp.int32, my_resets.shape, 1)
    first = jnp.min(jnp.where(my_resets != 0, positions, steps), axis=1).astype(jnp.float32)

    ends_local = local[:, -1, :]
    ends_hi = ends_local.astype(jnp.bfloat16)
    ends_lo = (ends_local - ends_hi.astype(jnp.float32)).astype(jnp.bfloat16)
    rows_sent = bh * sub
    lanes = -(-(2 * bh * width) // (rows_sent * 128)) * 128
    room = rows_sent * lanes - bh * width - bh
    lo_flat = ends_lo.reshape(-1)[:room]
    extra = jnp.concatenate(
        [ends_hi.reshape(-1), first.astype(jnp.bfloat16), lo_flat]
    )
    extra = jnp.pad(extra, (0, rows_sent * lanes - extra.shape[0])).reshape(rows_sent, lanes)
    states = jnp.swapaxes(local.astype(jnp.bfloat16).reshape(bh, ntm, sub, width), 0, 1)
    send = jnp.concatenate(
        [states.reshape(ntm, rows_sent, width), jnp.broadcast_to(extra[None], (ntm,) + extra.shape)],
        axis=2,
    )
    got = lax.all_to_all(send, "tm", split_axis=0, concat_axis=0, tiled=True)
    recv = jnp.swapaxes(got[:, :, :width].reshape(ntm, bh, sub, width), 0, 1)
    flat = got[:, :, width:].reshape(ntm, -1)
    got_hi = flat[:, : bh * width].astype(jnp.float32)
    firsts = flat[:, bh * width : bh * width + bh].astype(jnp.float32)
    got_lo = flat[:, bh * width + bh : bh * width + bh + lo_flat.shape[0]].astype(jnp.float32)
    got_lo = jnp.pad(got_lo, ((0, 0), (0, bh * width - lo_flat.shape[0])))
    gathered = (got_hi + got_lo).reshape(ntm, bh, width)
    ends = gathered

    nblocks = gathered.shape[0]
    whole_block = decays ** steps
    gain = jnp.where(firsts >= steps, 1.0, 0.0)[:, :, None] * whole_block
    total = ends
    offset = 1
    while offset < nblocks:
        gain_prev = jnp.concatenate([jnp.ones_like(gain[:offset]), gain[:-offset]], axis=0)
        total_prev = jnp.concatenate([jnp.zeros_like(total[:offset]), total[:-offset]], axis=0)
        total = gain * total_prev + total
        gain = gain * gain_prev
        offset *= 2
    carry = jnp.concatenate([jnp.zeros_like(total[:1]), total[:-1]], axis=0)

    t_glob = d * sub + lax.broadcasted_iota(jnp.int32, (sub,), 0)
    powers = decays[None, :] ** (t_glob[:, None] + 1).astype(jnp.float32)
    alive = t_glob[None, None, :].astype(jnp.float32) < jnp.swapaxes(firsts, 0, 1)[:, :, None]
    cum = jnp.where(alive[..., None], powers[None, None], 0.0)
    posterior = recv.astype(jnp.float32) + cum * jnp.swapaxes(carry, 0, 1)[:, :, None, :]

    _, blocks, _, horizon = actions.shape
    rows = bh * blocks * sub
    current = posterior.reshape(rows, width)
    my_actions = lax.dynamic_slice_in_dim(actions, m * bh, bh, 0).reshape(rows, horizon)
    table = jnp.concatenate([action_embed, emb_o], axis=1)
    table = jnp.pad(table, ((0, 128 - table.shape[0]), (0, 0)))
    one_hot = (
        jnp.swapaxes(my_actions, 0, 1)[:, :, None] == jnp.arange(128, dtype=jnp.int32)
    ).astype(jnp.bfloat16)
    vecs = jnp.stack([decays, scaling, norm_gain], axis=0)
    side = jnp.reshape(m, (1,)).astype(jnp.int32)
    keep_part, give_part = imagine(
        side, current, one_hot, vecs, readout_w, r_o, w_hidden, wh_o, table, w_out, wo_o,
        in_proj, ip_o,
    )
    got = partner(give_part)

    def arrange(part):
        return jnp.transpose(part.reshape(horizon, bh, blocks, sub, half), (1, 2, 3, 0, 4))

    mine, theirs = arrange(keep_part), arrange(got)
    first_half = jnp.where(m == 0, mine, theirs)
    second_half = jnp.where(m == 0, theirs, mine)
    return jnp.concatenate([first_half, second_half], axis=0)


def _imagine_kernel(
    side_ref, cur_ref, hot_ref, vec_ref, r_a, r_b, wh_a, wh_b, emb_ref, wo_a, wo_b, ip_a, ip_b,
    keep_ref, give_ref,
):
    horizon, rows, _ = hot_ref.shape
    half = r_a.shape[0]
    width = 2 * half
    tile = 256
    lead = side_ref[0] == 0

    def dot(a, b):
        return jnp.dot(a, b, preferred_element_type=jnp.float32)

    def chunk(c, carry):
        rs = pl.ds(pl.multiple_of(c * tile, tile), tile)
        cur_a = cur_ref[rs, :half]
        cur_b = cur_ref[rs, half:]
        for step in range(horizon):
            f = dot(cur_a.astype(jnp.bfloat16), r_a[...]).astype(jnp.bfloat16).astype(
                jnp.float32
            ) + dot(cur_b.astype(jnp.bfloat16), r_b[...]).astype(jnp.bfloat16).astype(jnp.float32)
            mean_sq = jnp.sum(f * f, axis=-1, keepdims=True) * (1.0 / width)
            normed = (f * lax.rsqrt(mean_sq + 1e-06) * vec_ref[2:3, :]).astype(jnp.bfloat16)
            hot = hot_ref[step, rs, :]
            pre_a = dot(normed, wh_a[...]) + dot(hot, emb_ref[:, :half])
            pre_b = dot(normed, wh_b[...]) + dot(hot, emb_ref[:, half:])
            hid_a = (pre_a * jax.nn.sigmoid(pre_a)).astype(jnp.bfloat16)
            hid_b = (pre_b * jax.nn.sigmoid(pre_b)).astype(jnp.bfloat16)
            lo = (dot(hid_a, wo_a[:, :half]) + dot(hid_b, wo_b[:, :half])).astype(jnp.bfloat16)
            hi = (dot(hid_a, wo_a[:, half:]) + dot(hid_b, wo_b[:, half:])).astype(jnp.bfloat16)
            keep_ref[step, rs, :] = jnp.where(lead, lo, hi)
            give_ref[step, rs, :] = jnp.where(lead, hi, lo)
            if step < horizon - 1:
                up_a = dot(lo, ip_a[:half, :]) + dot(hi, ip_a[half:, :])
                up_b = dot(lo, ip_b[:half, :]) + dot(hi, ip_b[half:, :])
                cur_a = vec_ref[0:1, :half] * cur_a + vec_ref[1:2, :half] * up_a
                cur_b = vec_ref[0:1, half:] * cur_b + vec_ref[1:2, half:] * up_b
        return carry

    lax.fori_loop(0, rows // tile, chunk, 0)


def imagine(side, current, one_hot, vecs, *weights):
    horizon, rows, _ = one_hot.shape
    half = weights[0].shape[0]
    out = jax.ShapeDtypeStruct((horizon, rows, half), jnp.bfloat16)
    vmem = pl.BlockSpec(memory_space=pltpu.VMEM)
    flops = 2 * rows * horizon * 4 * (2 * half) * (2 * half)
    return pl.pallas_call(
        _imagine_kernel,
        out_shape=(out, out),
        in_specs=[pl.BlockSpec(memory_space=pltpu.SMEM)] + [vmem] * (3 + len(weights)),
        out_specs=(vmem, vmem),
        compiler_params=pltpu.CompilerParams(vmem_limit_bytes=48 * 1024 * 1024),
        cost_estimate=pl.CostEstimate(
            flops=flops, bytes_accessed=16 * 1024 * 1024, transcendentals=rows * horizon * 2 * half
        ),
    )(side, current, one_hot, vecs, *weights)


def solution(mesh):
    in_specs = (
        P("rep", "tm", None),
        P("rep", "tm"),
        P("rep", None, "tm", None),
        P(None, "mp"),
        P(),
        P("mp", None),
        P(),
        P(None, "mp"),
        P(None, "mp"),
        P("mp", None),
    )
    out_specs = P("rep", None, "tm", None, "mp")
    return jax.shard_map(
        per_device, mesh=mesh, in_specs=in_specs, out_specs=out_specs, check_vma=False
    )
```

```python
import jax
import jax.numpy as jnp
from jax import lax
from jax.experimental import pallas as pl
from jax.experimental.pallas import tpu as pltpu
from jax.sharding import PartitionSpec as P


def _scan_kernel(x_ref, g_ref, o_ref):
    nb, steps, width = x_ref.shape

    def body(t, states):
        row = pl.ds(t, 1)
        new = []
        for b in range(nb):
            h = g_ref[b, row, :] * states[b] + x_ref[b, row, :]
            o_ref[b, row, :] = h
            new.append(h)
        return tuple(new)

    start = tuple(jnp.zeros((1, width), jnp.float32) for _ in range(nb))
    lax.fori_loop(0, steps, body, start, unroll=8)


def local_scan(driven, gates):
    size = driven.size
    return pl.pallas_call(
        _scan_kernel,
        out_shape=jax.ShapeDtypeStruct(driven.shape, jnp.float32),
        in_specs=[pl.BlockSpec(memory_space=pltpu.VMEM)] * 2,
        out_specs=pl.BlockSpec(memory_space=pltpu.VMEM),
        cost_estimate=pl.CostEstimate(flops=2 * size, bytes_accessed=12 * size, transcendentals=0),
    )(driven, gates)


def _scan_send_kernel(keep_ref, dec_ref, x_ref, send_ref, ends_ref, buf):
    nb, steps, width = x_ref.shape
    ntm, rows_sent, _ = send_ref.shape
    sub = rows_sent // nb
    dec = dec_ref[...]

    def body(t, states):
        row = pl.ds(t, 1)
        new = []
        for b in range(nb):
            h = (keep_ref[b, t] * dec) * states[b] + x_ref[b, row, :]
            buf[b, row, :] = h
            new.append(h)
        return tuple(new)

    start = tuple(jnp.zeros((1, width), jnp.float32) for _ in range(nb))
    final = lax.fori_loop(0, steps, body, start, unroll=8)
    for b in range(nb):
        ends_ref[pl.ds(b, 1), :] = final[b]
        for j in range(ntm):
            send_ref[j, pl.ds(b * sub, sub), :] = buf[b, pl.ds(j * sub, sub), :].astype(
                jnp.bfloat16
            )


def scan_send(keep, decays, driven, ntm):
    nb, steps, width = driven.shape
    sub = steps // ntm
    size = driven.size
    vmem = pl.BlockSpec(memory_space=pltpu.VMEM)
    return pl.pallas_call(
        _scan_send_kernel,
        out_shape=(
            jax.ShapeDtypeStruct((ntm, nb * sub, width), jnp.bfloat16),
            jax.ShapeDtypeStruct((nb, width), jnp.float32),
        ),
        in_specs=[pl.BlockSpec(memory_space=pltpu.SMEM), vmem, vmem],
        out_specs=(vmem, vmem),
        scratch_shapes=[pltpu.VMEM((nb, steps, width), jnp.float32)],
        cost_estimate=pl.CostEstimate(flops=3 * size, bytes_accessed=6 * size, transcendentals=0),
    )(keep, decays.reshape(1, width), driven)


def gather_blocks(value, axis, mine, count):
    if count & (count - 1):
        return lax.all_gather(value, axis)
    held = value[None]
    shift = 1
    while shift < count:
        pairs = [(i, (i + shift) % count) for i in range(count)]
        held = jnp.concatenate([held, lax.ppermute(held, axis, pairs)], axis=0)
        shift *= 2
    order = (mine - jnp.arange(count, dtype=jnp.int32)) % count
    return jnp.take(held, order, axis=0)


def per_device(
    inputs,
    resets,
    actions,
    in_proj,
    decay_rates,
    readout_w,
    norm_gain,
    w_hidden,
    action_embed,
    w_out,
):
    m = lax.axis_index("mp")
    d = lax.axis_index("tm")
    ntm = lax.axis_size("tm")
    swap = [(0, 1), (1, 0)]

    def partner(x):
        return lax.ppermute(x, "mp", swap)

    half = in_proj.shape[1]
    ip_o = partner(in_proj)
    r_o = partner(readout_w)
    wh_o = partner(w_hidden)
    wo_o = partner(w_out)
    emb_o = partner(action_embed)
    ip = jnp.concatenate([in_proj, ip_o], axis=1)

    rates = jnp.concatenate(
        [
            lax.dynamic_slice_in_dim(decay_rates, m * half, half),
            lax.dynamic_slice_in_dim(decay_rates, (1 - m) * half, half),
        ]
    )
    decays = jnp.exp(-rates)
    scaling = jnp.sqrt(1.0 - decays * decays)
    width = decays.shape[0]

    seqs, steps, feat = inputs.shape
    bh = seqs // 2
    x = lax.dynamic_slice_in_dim(inputs, m * bh, bh, 0)
    driven = (
        jnp.dot(x.reshape(bh * steps, feat), ip, preferred_element_type=jnp.float32).reshape(
            bh, steps, width
        )
        * scaling
    )
    my_resets = lax.dynamic_slice_in_dim(resets, m * bh, bh, 0)
    keep = (1 - my_resets).astype(jnp.float32)
    sub = steps // ntm
    if sub % 16 == 0:
        send_states, ends_local = scan_send(keep, decays, driven, ntm)
    else:
        local = local_scan(driven, keep[:, :, None] * decays)
        ends_local = local[:, -1, :]
        send_states = jnp.swapaxes(
            local.astype(jnp.bfloat16).reshape(bh, ntm, sub, width), 0, 1
        ).reshape(ntm, bh * sub, width)
    sub = steps // ntm
    positions = lax.broadcasted_iota(jnp.int32, my_resets.shape, 1)
    first = jnp.min(jnp.where(my_resets != 0, positions, steps), axis=1).astype(jnp.float32)

    ends_hi = ends_local.astype(jnp.bfloat16)
    ends_lo = (ends_local - ends_hi.astype(jnp.float32)).astype(jnp.bfloat16)
    rows_sent = bh * sub
    lanes = -(-(2 * bh * width) // (rows_sent * 128)) * 128
    room = rows_sent * lanes - bh * width - bh
    lo_flat = ends_lo.reshape(-1)[:room]
    extra = jnp.concatenate(
        [ends_hi.reshape(-1), first.astype(jnp.bfloat16), lo_flat]
    )
    extra = jnp.pad(extra, (0, rows_sent * lanes - extra.shape[0])).reshape(rows_sent, lanes)
    send = jnp.concatenate(
        [send_states, jnp.broadcast_to(extra[None], (ntm,) + extra.shape)],
        axis=2,
    )
    got = lax.all_to_all(send, "tm", split_axis=0, concat_axis=0, tiled=True)
    recv = jnp.swapaxes(got[:, :, :width].reshape(ntm, bh, sub, width), 0, 1)
    flat = got[:, :, width:].reshape(ntm, -1)
    got_hi = flat[:, : bh * width].astype(jnp.float32)
    firsts = flat[:, bh * width : bh * width + bh].astype(jnp.float32)
    got_lo = flat[:, bh * width + bh : bh * width + bh + lo_flat.shape[0]].astype(jnp.float32)
    got_lo = jnp.pad(got_lo, ((0, 0), (0, bh * width - lo_flat.shape[0])))
    gathered = (got_hi + got_lo).reshape(ntm, bh, width)
    ends = gathered

    nblocks = gathered.shape[0]
    whole_block = decays ** steps
    gain = jnp.where(firsts >= steps, 1.0, 0.0)[:, :, None] * whole_block
    total = ends
    offset = 1
    while offset < nblocks:
        gain_prev = jnp.concatenate([jnp.ones_like(gain[:offset]), gain[:-offset]], axis=0)
        total_prev = jnp.concatenate([jnp.zeros_like(total[:offset]), total[:-offset]], axis=0)
        total = gain * total_prev + total
        gain = gain * gain_prev
        offset *= 2
    carry = jnp.concatenate([jnp.zeros_like(total[:1]), total[:-1]], axis=0)

    t_glob = d * sub + lax.broadcasted_iota(jnp.int32, (sub,), 0)
    powers = decays[None, :] ** (t_glob[:, None] + 1).astype(jnp.float32)
    alive = t_glob[None, None, :].astype(jnp.float32) < jnp.swapaxes(firsts, 0, 1)[:, :, None]
    cum = jnp.where(alive[..., None], powers[None, None], 0.0)
    posterior = recv.astype(jnp.float32) + cum * jnp.swapaxes(carry, 0, 1)[:, :, None, :]

    _, blocks, _, horizon = actions.shape
    rows = bh * blocks * sub
    current = posterior.reshape(rows, width)
    my_actions = lax.dynamic_slice_in_dim(actions, m * bh, bh, 0).reshape(rows, horizon)
    table = jnp.concatenate([action_embed, emb_o], axis=1)
    table = jnp.pad(table, ((0, 128 - table.shape[0]), (0, 0)))
    one_hot = (
        jnp.swapaxes(my_actions, 0, 1)[:, :, None] == jnp.arange(128, dtype=jnp.int32)
    ).astype(jnp.bfloat16)
    vecs = jnp.stack([decays, scaling, norm_gain], axis=0)
    side = jnp.reshape(m, (1,)).astype(jnp.int32)
    keep_part, give_part = imagine(
        side, current, one_hot, vecs, readout_w, r_o, w_hidden, wh_o, table, w_out, wo_o,
        in_proj, ip_o,
    )
    got = partner(give_part)

    def arrange(part):
        return jnp.transpose(part.reshape(horizon, bh, blocks, sub, half), (1, 2, 3, 0, 4))

    mine, theirs = arrange(keep_part), arrange(got)
    first_half = jnp.where(m == 0, mine, theirs)
    second_half = jnp.where(m == 0, theirs, mine)
    return jnp.concatenate([first_half, second_half], axis=0)


def _imagine_kernel(
    side_ref, cur_ref, hot_ref, vec_ref, r_a, r_b, wh_a, wh_b, emb_ref, wo_a, wo_b, ip_a, ip_b,
    keep_ref, give_ref,
):
    horizon, rows, _ = hot_ref.shape
    half = r_a.shape[0]
    width = 2 * half
    tile = 256
    lead = side_ref[0] == 0

    def dot(a, b):
        return jnp.dot(a, b, preferred_element_type=jnp.float32)

    def chunk(c, carry):
        rs = pl.ds(pl.multiple_of(c * tile, tile), tile)
        cur_a = cur_ref[rs, :half]
        cur_b = cur_ref[rs, half:]
        for step in range(horizon):
            f = dot(cur_a.astype(jnp.bfloat16), r_a[...]).astype(jnp.bfloat16).astype(
                jnp.float32
            ) + dot(cur_b.astype(jnp.bfloat16), r_b[...]).astype(jnp.bfloat16).astype(jnp.float32)
            mean_sq = jnp.sum(f * f, axis=-1, keepdims=True) * (1.0 / width)
            normed = (f * lax.rsqrt(mean_sq + 1e-06) * vec_ref[2:3, :]).astype(jnp.bfloat16)
            hot = hot_ref[step, rs, :]
            pre_a = dot(normed, wh_a[...]) + dot(hot, emb_ref[:, :half])
            pre_b = dot(normed, wh_b[...]) + dot(hot, emb_ref[:, half:])
            hid_a = (pre_a * jax.nn.sigmoid(pre_a)).astype(jnp.bfloat16)
            hid_b = (pre_b * jax.nn.sigmoid(pre_b)).astype(jnp.bfloat16)
            lo = (dot(hid_a, wo_a[:, :half]) + dot(hid_b, wo_b[:, :half])).astype(jnp.bfloat16)
            hi = (dot(hid_a, wo_a[:, half:]) + dot(hid_b, wo_b[:, half:])).astype(jnp.bfloat16)
            keep_ref[step, rs, :] = jnp.where(lead, lo, hi)
            give_ref[step, rs, :] = jnp.where(lead, hi, lo)
            if step < horizon - 1:
                up_a = dot(lo, ip_a[:half, :]) + dot(hi, ip_a[half:, :])
                up_b = dot(lo, ip_b[:half, :]) + dot(hi, ip_b[half:, :])
                cur_a = vec_ref[0:1, :half] * cur_a + vec_ref[1:2, :half] * up_a
                cur_b = vec_ref[0:1, half:] * cur_b + vec_ref[1:2, half:] * up_b
        return carry

    lax.fori_loop(0, rows // tile, chunk, 0)


def imagine(side, current, one_hot, vecs, *weights):
    horizon, rows, _ = one_hot.shape
    half = weights[0].shape[0]
    out = jax.ShapeDtypeStruct((horizon, rows, half), jnp.bfloat16)
    vmem = pl.BlockSpec(memory_space=pltpu.VMEM)
    flops = 2 * rows * horizon * 4 * (2 * half) * (2 * half)
    return pl.pallas_call(
        _imagine_kernel,
        out_shape=(out, out),
        in_specs=[pl.BlockSpec(memory_space=pltpu.SMEM)] + [vmem] * (3 + len(weights)),
        out_specs=(vmem, vmem),
        compiler_params=pltpu.CompilerParams(vmem_limit_bytes=48 * 1024 * 1024),
        cost_estimate=pl.CostEstimate(
            flops=flops, bytes_accessed=16 * 1024 * 1024, transcendentals=rows * horizon * 2 * half
        ),
    )(side, current, one_hot, vecs, *weights)


def solution(mesh):
    in_specs = (
        P("rep", "tm", None),
        P("rep", "tm"),
        P("rep", None, "tm", None),
        P(None, "mp"),
        P(),
        P("mp", None),
        P(),
        P(None, "mp"),
        P(None, "mp"),
        P("mp", None),
    )
    out_specs = P("rep", None, "tm", None, "mp")
    return jax.shard_map(
        per_device, mesh=mesh, in_specs=in_specs, out_specs=out_specs, check_vma=False
    )
```

```python
import jax
import jax.numpy as jnp
from jax import lax
from jax.experimental import pallas as pl
from jax.experimental.pallas import tpu as pltpu
from jax.sharding import PartitionSpec as P


def _scan_kernel(x_ref, g_ref, o_ref):
    nb, steps, width = x_ref.shape

    def body(t, states):
        row = pl.ds(t, 1)
        new = []
        for b in range(nb):
            h = g_ref[b, row, :] * states[b] + x_ref[b, row, :]
            o_ref[b, row, :] = h
            new.append(h)
        return tuple(new)

    start = tuple(jnp.zeros((1, width), jnp.float32) for _ in range(nb))
    lax.fori_loop(0, steps, body, start, unroll=8)


def local_scan(driven, gates):
    size = driven.size
    return pl.pallas_call(
        _scan_kernel,
        out_shape=jax.ShapeDtypeStruct(driven.shape, jnp.float32),
        in_specs=[pl.BlockSpec(memory_space=pltpu.VMEM)] * 2,
        out_specs=pl.BlockSpec(memory_space=pltpu.VMEM),
        cost_estimate=pl.CostEstimate(flops=2 * size, bytes_accessed=12 * size, transcendentals=0),
    )(driven, gates)


def _scan_send_kernel(keep_ref, dec_ref, x_ref, send_ref, ends_ref, buf):
    nb, steps, width = x_ref.shape
    ntm, rows_sent, _ = send_ref.shape
    sub = rows_sent // nb
    dec = dec_ref[...]

    def body(t, states):
        row = pl.ds(t, 1)
        new = []
        for b in range(nb):
            h = (keep_ref[b, t] * dec) * states[b] + x_ref[b, row, :]
            buf[b, row, :] = h
            new.append(h)
        return tuple(new)

    start = tuple(jnp.zeros((1, width), jnp.float32) for _ in range(nb))
    final = lax.fori_loop(0, steps, body, start, unroll=8)
    for b in range(nb):
        ends_ref[pl.ds(b, 1), :] = final[b]
        for j in range(ntm):
            send_ref[j, pl.ds(b * sub, sub), pl.ds(0, width)] = buf[b, pl.ds(j * sub, sub), :].astype(
                jnp.bfloat16
            )


def scan_send(keep, decays, driven, ntm, spare):
    nb, steps, width = driven.shape
    sub = steps // ntm
    size = driven.size
    vmem = pl.BlockSpec(memory_space=pltpu.VMEM)
    return pl.pallas_call(
        _scan_send_kernel,
        out_shape=(
            jax.ShapeDtypeStruct((ntm, nb * sub, width + spare), jnp.bfloat16),
            jax.ShapeDtypeStruct((nb, width), jnp.float32),
        ),
        in_specs=[pl.BlockSpec(memory_space=pltpu.SMEM), vmem, vmem],
        out_specs=(vmem, vmem),
        scratch_shapes=[pltpu.VMEM((nb, steps, width), jnp.float32)],
        cost_estimate=pl.CostEstimate(flops=3 * size, bytes_accessed=6 * size, transcendentals=0),
    )(keep, decays.reshape(1, width), driven)


def gather_blocks(value, axis, mine, count):
    if count & (count - 1):
        return lax.all_gather(value, axis)
    held = value[None]
    shift = 1
    while shift < count:
        pairs = [(i, (i + shift) % count) for i in range(count)]
        held = jnp.concatenate([held, lax.ppermute(held, axis, pairs)], axis=0)
        shift *= 2
    order = (mine - jnp.arange(count, dtype=jnp.int32)) % count
    return jnp.take(held, order, axis=0)


def per_device(
    inputs,
    resets,
    actions,
    in_proj,
    decay_rates,
    readout_w,
    norm_gain,
    w_hidden,
    action_embed,
    w_out,
):
    m = lax.axis_index("mp")
    d = lax.axis_index("tm")
    ntm = lax.axis_size("tm")
    swap = [(0, 1), (1, 0)]

    def partner(x):
        return lax.ppermute(x, "mp", swap)

    half = in_proj.shape[1]
    ip_o = partner(in_proj)
    r_o = partner(readout_w)
    wh_o = partner(w_hidden)
    wo_o = partner(w_out)
    emb_o = partner(action_embed)
    ip = jnp.concatenate([in_proj, ip_o], axis=1)

    rates = jnp.concatenate(
        [
            lax.dynamic_slice_in_dim(decay_rates, m * half, half),
            lax.dynamic_slice_in_dim(decay_rates, (1 - m) * half, half),
        ]
    )
    decays = jnp.exp(-rates)
    scaling = jnp.sqrt(1.0 - decays * decays)
    width = decays.shape[0]

    seqs, steps, feat = inputs.shape
    bh = seqs // 2
    x = lax.dynamic_slice_in_dim(inputs, m * bh, bh, 0)
    driven = (
        jnp.dot(x.reshape(bh * steps, feat), ip, preferred_element_type=jnp.float32).reshape(
            bh, steps, width
        )
        * scaling
    )
    my_resets = lax.dynamic_slice_in_dim(resets, m * bh, bh, 0)
    keep = (1 - my_resets).astype(jnp.float32)
    sub = steps // ntm
    rows_sent = bh * sub
    lanes = -(-(2 * bh * width) // (rows_sent * 128)) * 128
    fused = sub % 16 == 0
    if fused:
        send_states, ends_local = scan_send(keep, decays, driven, ntm, lanes)
    else:
        local = local_scan(driven, keep[:, :, None] * decays)
        ends_local = local[:, -1, :]
        send_states = jnp.swapaxes(
            local.astype(jnp.bfloat16).reshape(bh, ntm, sub, width), 0, 1
        ).reshape(ntm, bh * sub, width)
    sub = steps // ntm
    positions = lax.broadcasted_iota(jnp.int32, my_resets.shape, 1)
    first = jnp.min(jnp.where(my_resets != 0, positions, steps), axis=1).astype(jnp.float32)

    ends_hi = ends_local.astype(jnp.bfloat16)
    ends_lo = (ends_local - ends_hi.astype(jnp.float32)).astype(jnp.bfloat16)
    room = rows_sent * lanes - bh * width - bh
    lo_flat = ends_lo.reshape(-1)[:room]
    extra = jnp.concatenate(
        [ends_hi.reshape(-1), first.astype(jnp.bfloat16), lo_flat]
    )
    extra = jnp.pad(extra, (0, rows_sent * lanes - extra.shape[0])).reshape(rows_sent, lanes)
    spread = jnp.broadcast_to(extra[None], (ntm,) + extra.shape)
    if fused:
        send = lax.dynamic_update_slice(send_states, spread, (0, 0, width))
    else:
        send = jnp.concatenate([send_states, spread], axis=2)
    got = lax.all_to_all(send, "tm", split_axis=0, concat_axis=0, tiled=True)
    recv = jnp.swapaxes(got[:, :, :width].reshape(ntm, bh, sub, width), 0, 1)
    flat = got[:, :, width:].reshape(ntm, -1)
    got_hi = flat[:, : bh * width].astype(jnp.float32)
    firsts = flat[:, bh * width : bh * width + bh].astype(jnp.float32)
    got_lo = flat[:, bh * width + bh : bh * width + bh + lo_flat.shape[0]].astype(jnp.float32)
    got_lo = jnp.pad(got_lo, ((0, 0), (0, bh * width - lo_flat.shape[0])))
    gathered = (got_hi + got_lo).reshape(ntm, bh, width)
    ends = gathered

    nblocks = gathered.shape[0]
    whole_block = decays ** steps
    gain = jnp.where(firsts >= steps, 1.0, 0.0)[:, :, None] * whole_block
    total = ends
    offset = 1
    while offset < nblocks:
        gain_prev = jnp.concatenate([jnp.ones_like(gain[:offset]), gain[:-offset]], axis=0)
        total_prev = jnp.concatenate([jnp.zeros_like(total[:offset]), total[:-offset]], axis=0)
        total = gain * total_prev + total
        gain = gain * gain_prev
        offset *= 2
    carry = jnp.concatenate([jnp.zeros_like(total[:1]), total[:-1]], axis=0)

    t_glob = d * sub + lax.broadcasted_iota(jnp.int32, (sub,), 0)
    powers = decays[None, :] ** (t_glob[:, None] + 1).astype(jnp.float32)
    alive = t_glob[None, None, :].astype(jnp.float32) < jnp.swapaxes(firsts, 0, 1)[:, :, None]
    cum = jnp.where(alive[..., None], powers[None, None], 0.0)
    posterior = recv.astype(jnp.float32) + cum * jnp.swapaxes(carry, 0, 1)[:, :, None, :]

    _, blocks, _, horizon = actions.shape
    rows = bh * blocks * sub
    current = posterior.reshape(rows, width)
    my_actions = lax.dynamic_slice_in_dim(actions, m * bh, bh, 0).reshape(rows, horizon)
    table = jnp.concatenate([action_embed, emb_o], axis=1)
    table = jnp.pad(table, ((0, 128 - table.shape[0]), (0, 0)))
    one_hot = (
        jnp.swapaxes(my_actions, 0, 1)[:, :, None] == jnp.arange(128, dtype=jnp.int32)
    ).astype(jnp.bfloat16)
    vecs = jnp.stack([decays, scaling, norm_gain], axis=0)
    side = jnp.reshape(m, (1,)).astype(jnp.int32)
    keep_part, give_part = imagine(
        side, current, one_hot, vecs, readout_w, r_o, w_hidden, wh_o, table, w_out, wo_o,
        in_proj, ip_o,
    )
    got = partner(give_part)

    def arrange(part):
        return jnp.transpose(part.reshape(horizon, bh, blocks, sub, half), (1, 2, 3, 0, 4))

    mine, theirs = arrange(keep_part), arrange(got)
    out = jnp.zeros((2 * bh,) + mine.shape[1:], mine.dtype)
    out = lax.dynamic_update_slice(out, mine, (m * bh, 0, 0, 0, 0))
    return lax.dynamic_update_slice(out, theirs, ((1 - m) * bh, 0, 0, 0, 0))


def _imagine_kernel(
    side_ref, cur_ref, hot_ref, vec_ref, r_a, r_b, wh_a, wh_b, emb_ref, wo_a, wo_b, ip_a, ip_b,
    keep_ref, give_ref,
):
    horizon, rows, _ = hot_ref.shape
    half = r_a.shape[0]
    width = 2 * half
    tile = 256
    lead = side_ref[0] == 0

    def dot(a, b):
        return jnp.dot(a, b, preferred_element_type=jnp.float32)

    def chunk(c, carry):
        rs = pl.ds(pl.multiple_of(c * tile, tile), tile)
        cur_a = cur_ref[rs, :half]
        cur_b = cur_ref[rs, half:]
        for step in range(horizon):
            f = dot(cur_a.astype(jnp.bfloat16), r_a[...]).astype(jnp.bfloat16).astype(
                jnp.float32
            ) + dot(cur_b.astype(jnp.bfloat16), r_b[...]).astype(jnp.bfloat16).astype(jnp.float32)
            mean_sq = jnp.sum(f * f, axis=-1, keepdims=True) * (1.0 / width)
            normed = (f * lax.rsqrt(mean_sq + 1e-06) * vec_ref[2:3, :]).astype(jnp.bfloat16)
            hot = hot_ref[step, rs, :]
            pre_a = dot(normed, wh_a[...]) + dot(hot, emb_ref[:, :half])
            pre_b = dot(normed, wh_b[...]) + dot(hot, emb_ref[:, half:])
            hid_a = (pre_a * jax.nn.sigmoid(pre_a)).astype(jnp.bfloat16)
            hid_b = (pre_b * jax.nn.sigmoid(pre_b)).astype(jnp.bfloat16)
            lo = (dot(hid_a, wo_a[:, :half]) + dot(hid_b, wo_b[:, :half])).astype(jnp.bfloat16)
            hi = (dot(hid_a, wo_a[:, half:]) + dot(hid_b, wo_b[:, half:])).astype(jnp.bfloat16)
            keep_ref[step, rs, :] = jnp.where(lead, lo, hi)
            give_ref[step, rs, :] = jnp.where(lead, hi, lo)
            if step < horizon - 1:
                up_a = dot(lo, ip_a[:half, :]) + dot(hi, ip_a[half:, :])
                up_b = dot(lo, ip_b[:half, :]) + dot(hi, ip_b[half:, :])
                cur_a = vec_ref[0:1, :half] * cur_a + vec_ref[1:2, :half] * up_a
                cur_b = vec_ref[0:1, half:] * cur_b + vec_ref[1:2, half:] * up_b
        return carry

    lax.fori_loop(0, rows // tile, chunk, 0)


def imagine(side, current, one_hot, vecs, *weights):
    horizon, rows, _ = one_hot.shape
    half = weights[0].shape[0]
    out = jax.ShapeDtypeStruct((horizon, rows, half), jnp.bfloat16)
    vmem = pl.BlockSpec(memory_space=pltpu.VMEM)
    flops = 2 * rows * horizon * 4 * (2 * half) * (2 * half)
    return pl.pallas_call(
        _imagine_kernel,
        out_shape=(out, out),
        in_specs=[pl.BlockSpec(memory_space=pltpu.SMEM)] + [vmem] * (3 + len(weights)),
        out_specs=(vmem, vmem),
        compiler_params=pltpu.CompilerParams(vmem_limit_bytes=48 * 1024 * 1024),
        cost_estimate=pl.CostEstimate(
            flops=flops, bytes_accessed=16 * 1024 * 1024, transcendentals=rows * horizon * 2 * half
        ),
    )(side, current, one_hot, vecs, *weights)


def solution(mesh):
    in_specs = (
        P("rep", "tm", None),
        P("rep", "tm"),
        P("rep", None, "tm", None),
        P(None, "mp"),
        P(),
        P("mp", None),
        P(),
        P(None, "mp"),
        P(None, "mp"),
        P("mp", None),
    )
    out_specs = P("rep", None, "tm", None, "mp")
    return jax.shard_map(
        per_device, mesh=mesh, in_specs=in_specs, out_specs=out_specs, check_vma=False
    )
```

```python
import jax
import jax.numpy as jnp
from jax import lax
from jax.experimental import pallas as pl
from jax.experimental.pallas import tpu as pltpu
from jax.sharding import PartitionSpec as P


def _scan_kernel(x_ref, g_ref, o_ref):
    nb, steps, width = x_ref.shape

    def body(t, states):
        row = pl.ds(t, 1)
        new = []
        for b in range(nb):
            h = g_ref[b, row, :] * states[b] + x_ref[b, row, :]
            o_ref[b, row, :] = h
            new.append(h)
        return tuple(new)

    start = tuple(jnp.zeros((1, width), jnp.float32) for _ in range(nb))
    lax.fori_loop(0, steps, body, start, unroll=8)


def local_scan(driven, gates):
    size = driven.size
    return pl.pallas_call(
        _scan_kernel,
        out_shape=jax.ShapeDtypeStruct(driven.shape, jnp.float32),
        in_specs=[pl.BlockSpec(memory_space=pltpu.VMEM)] * 2,
        out_specs=pl.BlockSpec(memory_space=pltpu.VMEM),
        cost_estimate=pl.CostEstimate(flops=2 * size, bytes_accessed=12 * size, transcendentals=0),
    )(driven, gates)


def _scan_send_kernel(keep_ref, dec_ref, xa_ref, xb_ref, send_ref, ends_ref, buf):
    nb, steps, half = xa_ref.shape
    width = 2 * half
    ntm, rows_sent, _ = send_ref.shape
    sub = rows_sent // nb
    dec_a = dec_ref[:, :half]
    dec_b = dec_ref[:, half:]

    def body(t, states):
        row = pl.ds(t, 1)
        new = []
        for b in range(nb):
            keep_now = keep_ref[b, t]
            ha = (keep_now * dec_a) * states[2 * b] + xa_ref[b, row, :]
            hb = (keep_now * dec_b) * states[2 * b + 1] + xb_ref[b, row, :]
            buf[b, row, pl.ds(0, half)] = ha
            buf[b, row, pl.ds(half, half)] = hb
            new += [ha, hb]
        return tuple(new)

    start = tuple(jnp.zeros((1, half), jnp.float32) for _ in range(2 * nb))
    final = lax.fori_loop(0, steps, body, start, unroll=8)
    for b in range(nb):
        ends_ref[pl.ds(b, 1), pl.ds(0, half)] = final[2 * b]
        ends_ref[pl.ds(b, 1), pl.ds(half, half)] = final[2 * b + 1]
        for j in range(ntm):
            send_ref[j, pl.ds(b * sub, sub), pl.ds(0, width)] = buf[b, pl.ds(j * sub, sub), :].astype(
                jnp.bfloat16
            )


def scan_send(keep, decays, driven_a, driven_b, ntm, spare):
    nb, steps, half = driven_a.shape
    width = 2 * half
    sub = steps // ntm
    size = 2 * driven_a.size
    vmem = pl.BlockSpec(memory_space=pltpu.VMEM)
    return pl.pallas_call(
        _scan_send_kernel,
        out_shape=(
            jax.ShapeDtypeStruct((ntm, nb * sub, width + spare), jnp.bfloat16),
            jax.ShapeDtypeStruct((nb, width), jnp.float32),
        ),
        in_specs=[pl.BlockSpec(memory_space=pltpu.SMEM), vmem, vmem, vmem],
        out_specs=(vmem, vmem),
        scratch_shapes=[pltpu.VMEM((nb, steps, width), jnp.float32)],
        cost_estimate=pl.CostEstimate(flops=3 * size, bytes_accessed=6 * size, transcendentals=0),
    )(keep, decays.reshape(1, width), driven_a, driven_b)


def gather_blocks(value, axis, mine, count):
    if count & (count - 1):
        return lax.all_gather(value, axis)
    held = value[None]
    shift = 1
    while shift < count:
        pairs = [(i, (i + shift) % count) for i in range(count)]
        held = jnp.concatenate([held, lax.ppermute(held, axis, pairs)], axis=0)
        shift *= 2
    order = (mine - jnp.arange(count, dtype=jnp.int32)) % count
    return jnp.take(held, order, axis=0)


def per_device(
    inputs,
    resets,
    actions,
    in_proj,
    decay_rates,
    readout_w,
    norm_gain,
    w_hidden,
    action_embed,
    w_out,
):
    m = lax.axis_index("mp")
    d = lax.axis_index("tm")
    ntm = lax.axis_size("tm")
    swap = [(0, 1), (1, 0)]

    def partner(x):
        return lax.ppermute(x, "mp", swap)

    half = in_proj.shape[1]
    ip_o = partner(in_proj)
    r_o = partner(readout_w)
    wh_o = partner(w_hidden)
    wo_o = partner(w_out)
    emb_o = partner(action_embed)
    ip = jnp.concatenate([in_proj, ip_o], axis=1)

    rates = jnp.concatenate(
        [
            lax.dynamic_slice_in_dim(decay_rates, m * half, half),
            lax.dynamic_slice_in_dim(decay_rates, (1 - m) * half, half),
        ]
    )
    decays = jnp.exp(-rates)
    scaling = jnp.sqrt(1.0 - decays * decays)
    width = decays.shape[0]

    seqs, steps, feat = inputs.shape
    bh = seqs // 2
    x = lax.dynamic_slice_in_dim(inputs, m * bh, bh, 0)
    driven = (
        jnp.dot(x.reshape(bh * steps, feat), ip, preferred_element_type=jnp.float32).reshape(
            bh, steps, width
        )
        * scaling
    )
    my_resets = lax.dynamic_slice_in_dim(resets, m * bh, bh, 0)
    keep = (1 - my_resets).astype(jnp.float32)
    sub = steps // ntm
    rows_sent = bh * sub
    lanes = -(-(2 * bh * width) // (rows_sent * 128)) * 128
    fused = sub % 16 == 0
    if fused:
        flat_x = x.reshape(bh * steps, feat)
        driven_a = jnp.dot(flat_x, in_proj, preferred_element_type=jnp.float32).reshape(
            bh, steps, half
        ) * scaling[:half]
        driven_b = jnp.dot(flat_x, ip_o, preferred_element_type=jnp.float32).reshape(
            bh, steps, half
        ) * scaling[half:]
        send_states, ends_local = scan_send(keep, decays, driven_a, driven_b, ntm, lanes)
    else:
        local = local_scan(driven, keep[:, :, None] * decays)
        ends_local = local[:, -1, :]
        send_states = jnp.swapaxes(
            local.astype(jnp.bfloat16).reshape(bh, ntm, sub, width), 0, 1
        ).reshape(ntm, bh * sub, width)
    sub = steps // ntm
    positions = lax.broadcasted_iota(jnp.int32, my_resets.shape, 1)
    first = jnp.min(jnp.where(my_resets != 0, positions, steps), axis=1).astype(jnp.float32)

    ends_hi = ends_local.astype(jnp.bfloat16)
    ends_lo = (ends_local - ends_hi.astype(jnp.float32)).astype(jnp.bfloat16)
    room = rows_sent * lanes - bh * width - bh
    lo_flat = ends_lo.reshape(-1)[:room]
    extra = jnp.concatenate(
        [ends_hi.reshape(-1), first.astype(jnp.bfloat16), lo_flat]
    )
    extra = jnp.pad(extra, (0, rows_sent * lanes - extra.shape[0])).reshape(rows_sent, lanes)
    spread = jnp.broadcast_to(extra[None], (ntm,) + extra.shape)
    if fused:
        send = lax.dynamic_update_slice(send_states, spread, (0, 0, width))
    else:
        send = jnp.concatenate([send_states, spread], axis=2)
    got = lax.all_to_all(send, "tm", split_axis=0, concat_axis=0, tiled=True)
    recv = jnp.swapaxes(got[:, :, :width].reshape(ntm, bh, sub, width), 0, 1)
    flat = got[:, :, width:].reshape(ntm, -1)
    got_hi = flat[:, : bh * width].astype(jnp.float32)
    firsts = flat[:, bh * width : bh * width + bh].astype(jnp.float32)
    got_lo = flat[:, bh * width + bh : bh * width + bh + lo_flat.shape[0]].astype(jnp.float32)
    got_lo = jnp.pad(got_lo, ((0, 0), (0, bh * width - lo_flat.shape[0])))
    gathered = (got_hi + got_lo).reshape(ntm, bh, width)
    ends = gathered

    nblocks = gathered.shape[0]
    whole_block = decays ** steps
    gain = jnp.where(firsts >= steps, 1.0, 0.0)[:, :, None] * whole_block
    total = ends
    offset = 1
    while offset < nblocks:
        gain_prev = jnp.concatenate([jnp.ones_like(gain[:offset]), gain[:-offset]], axis=0)
        total_prev = jnp.concatenate([jnp.zeros_like(total[:offset]), total[:-offset]], axis=0)
        total = gain * total_prev + total
        gain = gain * gain_prev
        offset *= 2
    carry = jnp.concatenate([jnp.zeros_like(total[:1]), total[:-1]], axis=0)

    t_glob = d * sub + lax.broadcasted_iota(jnp.int32, (sub,), 0)
    powers = decays[None, :] ** (t_glob[:, None] + 1).astype(jnp.float32)
    alive = t_glob[None, None, :].astype(jnp.float32) < jnp.swapaxes(firsts, 0, 1)[:, :, None]
    cum = jnp.where(alive[..., None], powers[None, None], 0.0)
    posterior = recv.astype(jnp.float32) + cum * jnp.swapaxes(carry, 0, 1)[:, :, None, :]

    _, blocks, _, horizon = actions.shape
    rows = bh * blocks * sub
    current = posterior.reshape(rows, width)
    my_actions = lax.dynamic_slice_in_dim(actions, m * bh, bh, 0).reshape(rows, horizon)
    table = jnp.concatenate([action_embed, emb_o], axis=1)
    table = jnp.pad(table, ((0, 128 - table.shape[0]), (0, 0)))
    one_hot = (
        jnp.swapaxes(my_actions, 0, 1)[:, :, None] == jnp.arange(128, dtype=jnp.int32)
    ).astype(jnp.bfloat16)
    vecs = jnp.stack([decays, scaling, norm_gain], axis=0)
    side = jnp.reshape(m, (1,)).astype(jnp.int32)
    keep_part, give_part = imagine(
        side, current, one_hot, vecs, readout_w, r_o, w_hidden, wh_o, table, w_out, wo_o,
        in_proj, ip_o,
    )
    got = partner(give_part)

    def arrange(part):
        return jnp.transpose(part.reshape(horizon, bh, blocks, sub, half), (1, 2, 3, 0, 4))

    mine, theirs = arrange(keep_part), arrange(got)
    out = jnp.zeros((2 * bh,) + mine.shape[1:], mine.dtype)
    out = lax.dynamic_update_slice(out, mine, (m * bh, 0, 0, 0, 0))
    return lax.dynamic_update_slice(out, theirs, ((1 - m) * bh, 0, 0, 0, 0))


def _imagine_kernel(
    side_ref, cur_ref, hot_ref, vec_ref, r_a, r_b, wh_a, wh_b, emb_ref, wo_a, wo_b, ip_a, ip_b,
    keep_ref, give_ref,
):
    horizon, rows, _ = hot_ref.shape
    half = r_a.shape[0]
    width = 2 * half
    tile = 256
    lead = side_ref[0] == 0

    def dot(a, b):
        return jnp.dot(a, b, preferred_element_type=jnp.float32)

    def chunk(c, carry):
        rs = pl.ds(pl.multiple_of(c * tile, tile), tile)
        cur_a = cur_ref[rs, :half]
        cur_b = cur_ref[rs, half:]
        for step in range(horizon):
            f = dot(cur_a.astype(jnp.bfloat16), r_a[...]).astype(jnp.bfloat16).astype(
                jnp.float32
            ) + dot(cur_b.astype(jnp.bfloat16), r_b[...]).astype(jnp.bfloat16).astype(jnp.float32)
            mean_sq = jnp.sum(f * f, axis=-1, keepdims=True) * (1.0 / width)
            normed = (f * lax.rsqrt(mean_sq + 1e-06) * vec_ref[2:3, :]).astype(jnp.bfloat16)
            hot = hot_ref[step, rs, :]
            pre_a = dot(normed, wh_a[...]) + dot(hot, emb_ref[:, :half])
            pre_b = dot(normed, wh_b[...]) + dot(hot, emb_ref[:, half:])
            hid_a = (pre_a * jax.nn.sigmoid(pre_a)).astype(jnp.bfloat16)
            hid_b = (pre_b * jax.nn.sigmoid(pre_b)).astype(jnp.bfloat16)
            lo = (dot(hid_a, wo_a[:, :half]) + dot(hid_b, wo_b[:, :half])).astype(jnp.bfloat16)
            hi = (dot(hid_a, wo_a[:, half:]) + dot(hid_b, wo_b[:, half:])).astype(jnp.bfloat16)
            keep_ref[step, rs, :] = jnp.where(lead, lo, hi)
            give_ref[step, rs, :] = jnp.where(lead, hi, lo)
            if step < horizon - 1:
                up_a = dot(lo, ip_a[:half, :]) + dot(hi, ip_a[half:, :])
                up_b = dot(lo, ip_b[:half, :]) + dot(hi, ip_b[half:, :])
                cur_a = vec_ref[0:1, :half] * cur_a + vec_ref[1:2, :half] * up_a
                cur_b = vec_ref[0:1, half:] * cur_b + vec_ref[1:2, half:] * up_b
        return carry

    lax.fori_loop(0, rows // tile, chunk, 0)


def imagine(side, current, one_hot, vecs, *weights):
    horizon, rows, _ = one_hot.shape
    half = weights[0].shape[0]
    out = jax.ShapeDtypeStruct((horizon, rows, half), jnp.bfloat16)
    vmem = pl.BlockSpec(memory_space=pltpu.VMEM)
    flops = 2 * rows * horizon * 4 * (2 * half) * (2 * half)
    return pl.pallas_call(
        _imagine_kernel,
        out_shape=(out, out),
        in_specs=[pl.BlockSpec(memory_space=pltpu.SMEM)] + [vmem] * (3 + len(weights)),
        out_specs=(vmem, vmem),
        compiler_params=pltpu.CompilerParams(vmem_limit_bytes=48 * 1024 * 1024),
        cost_estimate=pl.CostEstimate(
            flops=flops, bytes_accessed=16 * 1024 * 1024, transcendentals=rows * horizon * 2 * half
        ),
    )(side, current, one_hot, vecs, *weights)


def solution(mesh):
    in_specs = (
        P("rep", "tm", None),
        P("rep", "tm"),
        P("rep", None, "tm", None),
        P(None, "mp"),
        P(),
        P("mp", None),
        P(),
        P(None, "mp"),
        P(None, "mp"),
        P("mp", None),
    )
    out_specs = P("rep", None, "tm", None, "mp")
    return jax.shard_map(
        per_device, mesh=mesh, in_specs=in_specs, out_specs=out_specs, check_vma=False
    )
```

```python
import jax
import jax.numpy as jnp
from jax import lax
from jax.experimental import pallas as pl
from jax.experimental.pallas import tpu as pltpu
from jax.sharding import PartitionSpec as P


def _scan_kernel(x_ref, g_ref, o_ref):
    nb, steps, width = x_ref.shape

    def body(t, states):
        row = pl.ds(t, 1)
        new = []
        for b in range(nb):
            h = g_ref[b, row, :] * states[b] + x_ref[b, row, :]
            o_ref[b, row, :] = h
            new.append(h)
        return tuple(new)

    start = tuple(jnp.zeros((1, width), jnp.float32) for _ in range(nb))
    lax.fori_loop(0, steps, body, start, unroll=8)


def local_scan(driven, gates):
    size = driven.size
    return pl.pallas_call(
        _scan_kernel,
        out_shape=jax.ShapeDtypeStruct(driven.shape, jnp.float32),
        in_specs=[pl.BlockSpec(memory_space=pltpu.VMEM)] * 2,
        out_specs=pl.BlockSpec(memory_space=pltpu.VMEM),
        cost_estimate=pl.CostEstimate(flops=2 * size, bytes_accessed=12 * size, transcendentals=0),
    )(driven, gates)


def _scan_send_kernel(keep_ref, dec_ref, xa_ref, xb_ref, send_ref, ends_ref, buf):
    nb, steps, half = xa_ref.shape
    width = 2 * half
    ntm, rows_sent, _ = send_ref.shape
    sub = rows_sent // nb
    dec_a = dec_ref[:, :half]
    dec_b = dec_ref[:, half:]

    def body(t, states):
        row = pl.ds(t, 1)
        new = []
        for b in range(nb):
            keep_now = keep_ref[b, t]
            ha = (keep_now * dec_a) * states[2 * b] + xa_ref[b, row, :]
            hb = (keep_now * dec_b) * states[2 * b + 1] + xb_ref[b, row, :]
            buf[b, row, pl.ds(0, half)] = ha
            buf[b, row, pl.ds(half, half)] = hb
            new += [ha, hb]
        return tuple(new)

    start = tuple(jnp.zeros((1, half), jnp.float32) for _ in range(2 * nb))
    final = lax.fori_loop(0, steps, body, start, unroll=8)
    for b in range(nb):
        ends_ref[pl.ds(b, 1), pl.ds(0, half)] = final[2 * b]
        ends_ref[pl.ds(b, 1), pl.ds(half, half)] = final[2 * b + 1]
        for j in range(ntm):
            send_ref[j, pl.ds(b * sub, sub), pl.ds(0, width)] = buf[b, pl.ds(j * sub, sub), :].astype(
                jnp.bfloat16
            )


def scan_send(keep, decays, driven_a, driven_b, ntm, spare):
    nb, steps, half = driven_a.shape
    width = 2 * half
    sub = steps // ntm
    size = 2 * driven_a.size
    vmem = pl.BlockSpec(memory_space=pltpu.VMEM)
    return pl.pallas_call(
        _scan_send_kernel,
        out_shape=(
            jax.ShapeDtypeStruct((ntm, nb * sub, width + spare), jnp.bfloat16),
            jax.ShapeDtypeStruct((nb, width), jnp.float32),
        ),
        in_specs=[pl.BlockSpec(memory_space=pltpu.SMEM), vmem, vmem, vmem],
        out_specs=(vmem, vmem),
        scratch_shapes=[pltpu.VMEM((nb, steps, width), jnp.float32)],
        cost_estimate=pl.CostEstimate(flops=3 * size, bytes_accessed=6 * size, transcendentals=0),
    )(keep, decays.reshape(1, width), driven_a, driven_b)


def gather_blocks(value, axis, mine, count):
    if count & (count - 1):
        return lax.all_gather(value, axis)
    held = value[None]
    shift = 1
    while shift < count:
        pairs = [(i, (i + shift) % count) for i in range(count)]
        held = jnp.concatenate([held, lax.ppermute(held, axis, pairs)], axis=0)
        shift *= 2
    order = (mine - jnp.arange(count, dtype=jnp.int32)) % count
    return jnp.take(held, order, axis=0)


def per_device(
    inputs,
    resets,
    actions,
    in_proj,
    decay_rates,
    readout_w,
    norm_gain,
    w_hidden,
    action_embed,
    w_out,
):
    m = lax.axis_index("mp")
    d = lax.axis_index("tm")
    ntm = lax.axis_size("tm")
    swap = [(0, 1), (1, 0)]

    def partner(x):
        return lax.ppermute(x, "mp", swap)

    half = in_proj.shape[1]
    ip_o = partner(in_proj)
    r_o = partner(readout_w)
    wh_o = partner(w_hidden)
    wo_o = partner(w_out)
    emb_o = partner(action_embed)
    ip = jnp.concatenate([in_proj, ip_o], axis=1)

    rates = jnp.concatenate(
        [
            lax.dynamic_slice_in_dim(decay_rates, m * half, half),
            lax.dynamic_slice_in_dim(decay_rates, (1 - m) * half, half),
        ]
    )
    decays = jnp.exp(-rates)
    scaling = jnp.sqrt(1.0 - decays * decays)
    width = decays.shape[0]

    seqs, steps, feat = inputs.shape
    bh = seqs // 2
    x = lax.dynamic_slice_in_dim(inputs, m * bh, bh, 0)
    driven = (
        jnp.dot(x.reshape(bh * steps, feat), ip, preferred_element_type=jnp.float32).reshape(
            bh, steps, width
        )
        * scaling
    )
    my_resets = lax.dynamic_slice_in_dim(resets, m * bh, bh, 0)
    keep = (1 - my_resets).astype(jnp.float32)
    sub = steps // ntm
    rows_sent = bh * sub
    lanes = -(-(2 * bh * width) // (rows_sent * 128)) * 128
    fused = sub % 16 == 0
    if fused:
        flat_x = x.reshape(bh * steps, feat)
        driven_a = jnp.dot(flat_x, in_proj, preferred_element_type=jnp.float32).reshape(
            bh, steps, half
        ) * scaling[:half]
        driven_b = jnp.dot(flat_x, ip_o, preferred_element_type=jnp.float32).reshape(
            bh, steps, half
        ) * scaling[half:]
        send_states, ends_local = scan_send(keep, decays, driven_a, driven_b, ntm, lanes)
    else:
        local = local_scan(driven, keep[:, :, None] * decays)
        ends_local = local[:, -1, :]
        send_states = jnp.swapaxes(
            local.astype(jnp.bfloat16).reshape(bh, ntm, sub, width), 0, 1
        ).reshape(ntm, bh * sub, width)
    sub = steps // ntm
    positions = lax.broadcasted_iota(jnp.int32, my_resets.shape, 1)
    first = jnp.min(jnp.where(my_resets != 0, positions, steps), axis=1).astype(jnp.float32)

    ends_hi = ends_local.astype(jnp.bfloat16)
    ends_lo = (ends_local - ends_hi.astype(jnp.float32)).astype(jnp.bfloat16)
    room = rows_sent * lanes - bh * width - bh
    lo_flat = ends_lo.reshape(-1)[:room]
    extra = jnp.concatenate(
        [ends_hi.reshape(-1), first.astype(jnp.bfloat16), lo_flat]
    )
    extra = jnp.pad(extra, (0, rows_sent * lanes - extra.shape[0])).reshape(rows_sent, lanes)
    spread = jnp.broadcast_to(extra[None], (ntm,) + extra.shape)
    if fused:
        send = lax.dynamic_update_slice(send_states, spread, (0, 0, width))
    else:
        send = jnp.concatenate([send_states, spread], axis=2)
    got = lax.all_to_all(send, "tm", split_axis=0, concat_axis=0, tiled=True)
    recv = jnp.swapaxes(got[:, :, :width].reshape(ntm, bh, sub, width), 0, 1)
    flat = got[:, :, width:].reshape(ntm, -1)
    got_hi = flat[:, : bh * width].astype(jnp.float32)
    firsts = flat[:, bh * width : bh * width + bh].astype(jnp.float32)
    got_lo = flat[:, bh * width + bh : bh * width + bh + lo_flat.shape[0]].astype(jnp.float32)
    got_lo = jnp.pad(got_lo, ((0, 0), (0, bh * width - lo_flat.shape[0])))
    gathered = (got_hi + got_lo).reshape(ntm, bh, width)
    ends = gathered

    nblocks = gathered.shape[0]
    whole_block = decays ** steps
    gain = jnp.where(firsts >= steps, 1.0, 0.0)[:, :, None] * whole_block
    total = ends
    offset = 1
    while offset < nblocks:
        gain_prev = jnp.concatenate([jnp.ones_like(gain[:offset]), gain[:-offset]], axis=0)
        total_prev = jnp.concatenate([jnp.zeros_like(total[:offset]), total[:-offset]], axis=0)
        total = gain * total_prev + total
        gain = gain * gain_prev
        offset *= 2
    carry = jnp.concatenate([jnp.zeros_like(total[:1]), total[:-1]], axis=0)

    t_glob = d * sub + lax.broadcasted_iota(jnp.int32, (sub,), 0)
    powers = decays[None, :] ** (t_glob[:, None] + 1).astype(jnp.float32)
    alive = t_glob[None, None, :].astype(jnp.float32) < jnp.swapaxes(firsts, 0, 1)[:, :, None]
    cum = jnp.where(alive[..., None], powers[None, None], 0.0)
    posterior = recv.astype(jnp.float32) + cum * jnp.swapaxes(carry, 0, 1)[:, :, None, :]

    _, blocks, _, horizon = actions.shape
    rows = bh * blocks * sub
    current = posterior.reshape(rows, width)
    my_actions = lax.dynamic_slice_in_dim(actions, m * bh, bh, 0).reshape(rows, horizon)
    table = jnp.concatenate([action_embed, emb_o], axis=1)
    table = jnp.pad(table, ((0, 128 - table.shape[0]), (0, 0)))
    one_hot = (
        jnp.swapaxes(my_actions, 0, 1)[:, :, None] == jnp.arange(128, dtype=jnp.int32)
    ).astype(jnp.bfloat16)
    vecs = jnp.stack([decays, scaling, norm_gain], axis=0)
    side = jnp.reshape(m, (1,)).astype(jnp.int32)
    keep_part, give_part = imagine(
        side, current, one_hot, vecs, readout_w, r_o, w_hidden, wh_o, table, w_out, wo_o,
        in_proj, ip_o,
    )
    got = partner(give_part)

    def arrange(part):
        return jnp.transpose(part.reshape(horizon, bh, blocks, sub, half), (1, 2, 3, 0, 4))

    mine, theirs = arrange(keep_part), arrange(got)
    out = jnp.zeros((2 * bh,) + mine.shape[1:], mine.dtype)
    out = lax.dynamic_update_slice(out, mine, (m * bh, 0, 0, 0, 0))
    return lax.dynamic_update_slice(out, theirs, ((1 - m) * bh, 0, 0, 0, 0))


def _imagine_kernel(
    side_ref, cur_ref, hot_ref, vec_ref, r_a, r_b, wh_a, wh_b, emb_ref, wo_a, wo_b, ip_a, ip_b,
    keep_ref, give_ref,
):
    horizon, rows, _ = hot_ref.shape
    half = r_a.shape[0]
    width = 2 * half
    tile = 256
    lead = side_ref[0] == 0

    def dot(a, b):
        return jnp.dot(a, b, preferred_element_type=jnp.float32)

    def chunk(c, carry):
        rs = pl.ds(pl.multiple_of(c * tile, tile), tile)
        cur_a = cur_ref[rs, :half]
        cur_b = cur_ref[rs, half:]
        for step in range(horizon):
            f = dot(cur_a.astype(jnp.bfloat16), r_a[...]).astype(jnp.bfloat16).astype(
                jnp.float32
            ) + dot(cur_b.astype(jnp.bfloat16), r_b[...]).astype(jnp.bfloat16).astype(jnp.float32)
            mean_sq = jnp.sum(f * f, axis=-1, keepdims=True) * (1.0 / width)
            normed = (f * lax.rsqrt(mean_sq + 1e-06) * vec_ref[2:3, :]).astype(jnp.bfloat16)
            hot = hot_ref[step, rs, :]
            pre_a = dot(normed, wh_a[...]) + dot(hot, emb_ref[:, :half])
            pre_b = dot(normed, wh_b[...]) + dot(hot, emb_ref[:, half:])
            hid_a = (0.5 * pre_a * (1.0 + jnp.tanh(0.5 * pre_a))).astype(jnp.bfloat16)
            hid_b = (0.5 * pre_b * (1.0 + jnp.tanh(0.5 * pre_b))).astype(jnp.bfloat16)
            lo = (dot(hid_a, wo_a[:, :half]) + dot(hid_b, wo_b[:, :half])).astype(jnp.bfloat16)
            hi = (dot(hid_a, wo_a[:, half:]) + dot(hid_b, wo_b[:, half:])).astype(jnp.bfloat16)
            keep_ref[step, rs, :] = jnp.where(lead, lo, hi)
            give_ref[step, rs, :] = jnp.where(lead, hi, lo)
            if step < horizon - 1:
                up_a = dot(lo, ip_a[:half, :]) + dot(hi, ip_a[half:, :])
                up_b = dot(lo, ip_b[:half, :]) + dot(hi, ip_b[half:, :])
                cur_a = vec_ref[0:1, :half] * cur_a + vec_ref[1:2, :half] * up_a
                cur_b = vec_ref[0:1, half:] * cur_b + vec_ref[1:2, half:] * up_b
        return carry

    lax.fori_loop(0, rows // tile, chunk, 0)


def imagine(side, current, one_hot, vecs, *weights):
    horizon, rows, _ = one_hot.shape
    half = weights[0].shape[0]
    out = jax.ShapeDtypeStruct((horizon, rows, half), jnp.bfloat16)
    vmem = pl.BlockSpec(memory_space=pltpu.VMEM)
    flops = 2 * rows * horizon * 4 * (2 * half) * (2 * half)
    return pl.pallas_call(
        _imagine_kernel,
        out_shape=(out, out),
        in_specs=[pl.BlockSpec(memory_space=pltpu.SMEM)] + [vmem] * (3 + len(weights)),
        out_specs=(vmem, vmem),
        compiler_params=pltpu.CompilerParams(vmem_limit_bytes=48 * 1024 * 1024),
        cost_estimate=pl.CostEstimate(
            flops=flops, bytes_accessed=16 * 1024 * 1024, transcendentals=rows * horizon * 2 * half
        ),
    )(side, current, one_hot, vecs, *weights)


def solution(mesh):
    in_specs = (
        P("rep", "tm", None),
        P("rep", "tm"),
        P("rep", None, "tm", None),
        P(None, "mp"),
        P(),
        P("mp", None),
        P(),
        P(None, "mp"),
        P(None, "mp"),
        P("mp", None),
    )
    out_specs = P("rep", None, "tm", None, "mp")
    return jax.shard_map(
        per_device, mesh=mesh, in_specs=in_specs, out_specs=out_specs, check_vma=False
    )
```

```python
import jax
import jax.numpy as jnp
from jax import lax
from jax.experimental import pallas as pl
from jax.experimental.pallas import tpu as pltpu
from jax.sharding import PartitionSpec as P


def _scan_kernel(x_ref, g_ref, o_ref):
    nb, steps, width = x_ref.shape

    def body(t, states):
        row = pl.ds(t, 1)
        new = []
        for b in range(nb):
            h = g_ref[b, row, :] * states[b] + x_ref[b, row, :]
            o_ref[b, row, :] = h
            new.append(h)
        return tuple(new)

    start = tuple(jnp.zeros((1, width), jnp.float32) for _ in range(nb))
    lax.fori_loop(0, steps, body, start, unroll=8)


def local_scan(driven, gates):
    size = driven.size
    return pl.pallas_call(
        _scan_kernel,
        out_shape=jax.ShapeDtypeStruct(driven.shape, jnp.float32),
        in_specs=[pl.BlockSpec(memory_space=pltpu.VMEM)] * 2,
        out_specs=pl.BlockSpec(memory_space=pltpu.VMEM),
        cost_estimate=pl.CostEstimate(flops=2 * size, bytes_accessed=12 * size, transcendentals=0),
    )(driven, gates)


def _scan_send_kernel(keep_ref, dec_ref, xa_ref, xb_ref, send_ref, ends_ref, buf):
    nb, steps, half = xa_ref.shape
    width = 2 * half
    ntm, rows_sent, _ = send_ref.shape
    sub = rows_sent // nb
    dec_a = dec_ref[:, :half]
    dec_b = dec_ref[:, half:]

    def body(t, states):
        row = pl.ds(t, 1)
        new = []
        for b in range(nb):
            keep_now = keep_ref[b, t]
            ha = (keep_now * dec_a) * states[2 * b] + xa_ref[b, row, :]
            hb = (keep_now * dec_b) * states[2 * b + 1] + xb_ref[b, row, :]
            buf[b, row, pl.ds(0, half)] = ha
            buf[b, row, pl.ds(half, half)] = hb
            new += [ha, hb]
        return tuple(new)

    start = tuple(jnp.zeros((1, half), jnp.float32) for _ in range(2 * nb))
    final = lax.fori_loop(0, steps, body, start, unroll=16)
    for b in range(nb):
        ends_ref[pl.ds(b, 1), pl.ds(0, half)] = final[2 * b]
        ends_ref[pl.ds(b, 1), pl.ds(half, half)] = final[2 * b + 1]
        for j in range(ntm):
            send_ref[j, pl.ds(b * sub, sub), pl.ds(0, width)] = buf[b, pl.ds(j * sub, sub), :].astype(
                jnp.bfloat16
            )


def scan_send(keep, decays, driven_a, driven_b, ntm, spare):
    nb, steps, half = driven_a.shape
    width = 2 * half
    sub = steps // ntm
    size = 2 * driven_a.size
    vmem = pl.BlockSpec(memory_space=pltpu.VMEM)
    return pl.pallas_call(
        _scan_send_kernel,
        out_shape=(
            jax.ShapeDtypeStruct((ntm, nb * sub, width + spare), jnp.bfloat16),
            jax.ShapeDtypeStruct((nb, width), jnp.float32),
        ),
        in_specs=[pl.BlockSpec(memory_space=pltpu.SMEM), vmem, vmem, vmem],
        out_specs=(vmem, vmem),
        scratch_shapes=[pltpu.VMEM((nb, steps, width), jnp.float32)],
        cost_estimate=pl.CostEstimate(flops=3 * size, bytes_accessed=6 * size, transcendentals=0),
    )(keep, decays.reshape(1, width), driven_a, driven_b)


def gather_blocks(value, axis, mine, count):
    if count & (count - 1):
        return lax.all_gather(value, axis)
    held = value[None]
    shift = 1
    while shift < count:
        pairs = [(i, (i + shift) % count) for i in range(count)]
        held = jnp.concatenate([held, lax.ppermute(held, axis, pairs)], axis=0)
        shift *= 2
    order = (mine - jnp.arange(count, dtype=jnp.int32)) % count
    return jnp.take(held, order, axis=0)


def per_device(
    inputs,
    resets,
    actions,
    in_proj,
    decay_rates,
    readout_w,
    norm_gain,
    w_hidden,
    action_embed,
    w_out,
):
    m = lax.axis_index("mp")
    d = lax.axis_index("tm")
    ntm = lax.axis_size("tm")
    swap = [(0, 1), (1, 0)]

    def partner(x):
        return lax.ppermute(x, "mp", swap)

    half = in_proj.shape[1]
    ip_o = partner(in_proj)
    r_o = partner(readout_w)
    wh_o = partner(w_hidden)
    wo_o = partner(w_out)
    emb_o = partner(action_embed)
    ip = jnp.concatenate([in_proj, ip_o], axis=1)

    rates = jnp.concatenate(
        [
            lax.dynamic_slice_in_dim(decay_rates, m * half, half),
            lax.dynamic_slice_in_dim(decay_rates, (1 - m) * half, half),
        ]
    )
    decays = jnp.exp(-rates)
    scaling = jnp.sqrt(1.0 - decays * decays)
    width = decays.shape[0]

    seqs, steps, feat = inputs.shape
    bh = seqs // 2
    x = lax.dynamic_slice_in_dim(inputs, m * bh, bh, 0)
    driven = (
        jnp.dot(x.reshape(bh * steps, feat), ip, preferred_element_type=jnp.float32).reshape(
            bh, steps, width
        )
        * scaling
    )
    my_resets = lax.dynamic_slice_in_dim(resets, m * bh, bh, 0)
    keep = (1 - my_resets).astype(jnp.float32)
    sub = steps // ntm
    rows_sent = bh * sub
    lanes = -(-(2 * bh * width) // (rows_sent * 128)) * 128
    fused = sub % 16 == 0
    if fused:
        flat_x = x.reshape(bh * steps, feat)
        driven_a = jnp.dot(flat_x, in_proj, preferred_element_type=jnp.float32).reshape(
            bh, steps, half
        ) * scaling[:half]
        driven_b = jnp.dot(flat_x, ip_o, preferred_element_type=jnp.float32).reshape(
            bh, steps, half
        ) * scaling[half:]
        send_states, ends_local = scan_send(keep, decays, driven_a, driven_b, ntm, lanes)
    else:
        local = local_scan(driven, keep[:, :, None] * decays)
        ends_local = local[:, -1, :]
        send_states = jnp.swapaxes(
            local.astype(jnp.bfloat16).reshape(bh, ntm, sub, width), 0, 1
        ).reshape(ntm, bh * sub, width)
    sub = steps // ntm
    positions = lax.broadcasted_iota(jnp.int32, my_resets.shape, 1)
    first = jnp.min(jnp.where(my_resets != 0, positions, steps), axis=1).astype(jnp.float32)

    ends_hi = ends_local.astype(jnp.bfloat16)
    ends_lo = (ends_local - ends_hi.astype(jnp.float32)).astype(jnp.bfloat16)
    room = rows_sent * lanes - bh * width - bh
    lo_flat = ends_lo.reshape(-1)[:room]
    extra = jnp.concatenate(
        [ends_hi.reshape(-1), first.astype(jnp.bfloat16), lo_flat]
    )
    extra = jnp.pad(extra, (0, rows_sent * lanes - extra.shape[0])).reshape(rows_sent, lanes)
    spread = jnp.broadcast_to(extra[None], (ntm,) + extra.shape)
    if fused:
        send = lax.dynamic_update_slice(send_states, spread, (0, 0, width))
    else:
        send = jnp.concatenate([send_states, spread], axis=2)
    got = lax.all_to_all(send, "tm", split_axis=0, concat_axis=0, tiled=True)
    recv = jnp.swapaxes(got[:, :, :width].reshape(ntm, bh, sub, width), 0, 1)
    flat = got[:, :, width:].reshape(ntm, -1)
    got_hi = flat[:, : bh * width].astype(jnp.float32)
    firsts = flat[:, bh * width : bh * width + bh].astype(jnp.float32)
    got_lo = flat[:, bh * width + bh : bh * width + bh + lo_flat.shape[0]].astype(jnp.float32)
    got_lo = jnp.pad(got_lo, ((0, 0), (0, bh * width - lo_flat.shape[0])))
    gathered = (got_hi + got_lo).reshape(ntm, bh, width)
    ends = gathered

    nblocks = gathered.shape[0]
    whole_block = decays ** steps
    gain = jnp.where(firsts >= steps, 1.0, 0.0)[:, :, None] * whole_block
    total = ends
    offset = 1
    while offset < nblocks:
        gain_prev = jnp.concatenate([jnp.ones_like(gain[:offset]), gain[:-offset]], axis=0)
        total_prev = jnp.concatenate([jnp.zeros_like(total[:offset]), total[:-offset]], axis=0)
        total = gain * total_prev + total
        gain = gain * gain_prev
        offset *= 2
    carry = jnp.concatenate([jnp.zeros_like(total[:1]), total[:-1]], axis=0)

    t_glob = d * sub + lax.broadcasted_iota(jnp.int32, (sub,), 0)
    powers = decays[None, :] ** (t_glob[:, None] + 1).astype(jnp.float32)
    alive = t_glob[None, None, :].astype(jnp.float32) < jnp.swapaxes(firsts, 0, 1)[:, :, None]
    cum = jnp.where(alive[..., None], powers[None, None], 0.0)
    posterior = recv.astype(jnp.float32) + cum * jnp.swapaxes(carry, 0, 1)[:, :, None, :]

    _, blocks, _, horizon = actions.shape
    rows = bh * blocks * sub
    current = posterior.reshape(rows, width)
    my_actions = lax.dynamic_slice_in_dim(actions, m * bh, bh, 0).reshape(rows, horizon)
    table = jnp.concatenate([action_embed, emb_o], axis=1)
    table = jnp.pad(table, ((0, 128 - table.shape[0]), (0, 0)))
    one_hot = (
        jnp.swapaxes(my_actions, 0, 1)[:, :, None] == jnp.arange(128, dtype=jnp.int32)
    ).astype(jnp.bfloat16)
    vecs = jnp.stack([decays, scaling, norm_gain], axis=0)
    side = jnp.reshape(m, (1,)).astype(jnp.int32)
    keep_part, give_part = imagine(
        side, current, one_hot, vecs, readout_w, r_o, w_hidden, wh_o, table, w_out, wo_o,
        in_proj, ip_o,
    )
    got = partner(give_part)

    def arrange(part):
        return jnp.transpose(part.reshape(horizon, bh, blocks, sub, half), (1, 2, 3, 0, 4))

    mine, theirs = arrange(keep_part), arrange(got)
    out = jnp.zeros((2 * bh,) + mine.shape[1:], mine.dtype)
    out = lax.dynamic_update_slice(out, mine, (m * bh, 0, 0, 0, 0))
    return lax.dynamic_update_slice(out, theirs, ((1 - m) * bh, 0, 0, 0, 0))


def _imagine_kernel(
    side_ref, cur_ref, hot_ref, vec_ref, r_a, r_b, wh_a, wh_b, emb_ref, wo_a, wo_b, ip_a, ip_b,
    keep_ref, give_ref,
):
    horizon, rows, _ = hot_ref.shape
    half = r_a.shape[0]
    width = 2 * half
    tile = 256
    lead = side_ref[0] == 0

    def dot(a, b):
        return jnp.dot(a, b, preferred_element_type=jnp.float32)

    def chunk(c, carry):
        rs = pl.ds(pl.multiple_of(c * tile, tile), tile)
        cur_a = cur_ref[rs, :half]
        cur_b = cur_ref[rs, half:]
        for step in range(horizon):
            f = dot(cur_a.astype(jnp.bfloat16), r_a[...]).astype(jnp.bfloat16).astype(
                jnp.float32
            ) + dot(cur_b.astype(jnp.bfloat16), r_b[...]).astype(jnp.bfloat16).astype(jnp.float32)
            mean_sq = jnp.sum(f * f, axis=-1, keepdims=True) * (1.0 / width)
            normed = (f * lax.rsqrt(mean_sq + 1e-06) * vec_ref[2:3, :]).astype(jnp.bfloat16)
            hot = hot_ref[step, rs, :]
            pre_a = dot(normed, wh_a[...]) + dot(hot, emb_ref[:, :half])
            pre_b = dot(normed, wh_b[...]) + dot(hot, emb_ref[:, half:])
            hid_a = (pre_a * jax.nn.sigmoid(pre_a)).astype(jnp.bfloat16)
            hid_b = (pre_b * jax.nn.sigmoid(pre_b)).astype(jnp.bfloat16)
            lo = (dot(hid_a, wo_a[:, :half]) + dot(hid_b, wo_b[:, :half])).astype(jnp.bfloat16)
            hi = (dot(hid_a, wo_a[:, half:]) + dot(hid_b, wo_b[:, half:])).astype(jnp.bfloat16)
            keep_ref[step, rs, :] = jnp.where(lead, lo, hi)
            give_ref[step, rs, :] = jnp.where(lead, hi, lo)
            if step < horizon - 1:
                up_a = dot(lo, ip_a[:half, :]) + dot(hi, ip_a[half:, :])
                up_b = dot(lo, ip_b[:half, :]) + dot(hi, ip_b[half:, :])
                cur_a = vec_ref[0:1, :half] * cur_a + vec_ref[1:2, :half] * up_a
                cur_b = vec_ref[0:1, half:] * cur_b + vec_ref[1:2, half:] * up_b
        return carry

    lax.fori_loop(0, rows // tile, chunk, 0)


def imagine(side, current, one_hot, vecs, *weights):
    horizon, rows, _ = one_hot.shape
    half = weights[0].shape[0]
    out = jax.ShapeDtypeStruct((horizon, rows, half), jnp.bfloat16)
    vmem = pl.BlockSpec(memory_space=pltpu.VMEM)
    flops = 2 * rows * horizon * 4 * (2 * half) * (2 * half)
    return pl.pallas_call(
        _imagine_kernel,
        out_shape=(out, out),
        in_specs=[pl.BlockSpec(memory_space=pltpu.SMEM)] + [vmem] * (3 + len(weights)),
        out_specs=(vmem, vmem),
        compiler_params=pltpu.CompilerParams(vmem_limit_bytes=48 * 1024 * 1024),
        cost_estimate=pl.CostEstimate(
            flops=flops, bytes_accessed=16 * 1024 * 1024, transcendentals=rows * horizon * 2 * half
        ),
    )(side, current, one_hot, vecs, *weights)


def solution(mesh):
    in_specs = (
        P("rep", "tm", None),
        P("rep", "tm"),
        P("rep", None, "tm", None),
        P(None, "mp"),
        P(),
        P("mp", None),
        P(),
        P(None, "mp"),
        P(None, "mp"),
        P("mp", None),
    )
    out_specs = P("rep", None, "tm", None, "mp")
    return jax.shard_map(
        per_device, mesh=mesh, in_specs=in_specs, out_specs=out_specs, check_vma=False
    )
```
